1024 devices in a mesh: region: 32 (over x, z_hi, core), group: 32 (over z_lo, y).
Axes of the slice: x: 4, y: 4, z: 32 (z_hi: 4, z_lo: 8; z = z_hi * 8 + z_lo), core: 2. Of those that a mesh axis runs over, the one named last changes fastest.
Arguments:
- right_side: float32 [216, 393216], P(None, ('region', 'group')), may hold values from -4 to 4
- stiff_fine: float32 [216, 216], replicated
- smooth_fine: float32 [216, 216], replicated
- restrict_fine: float32 [27, 216], replicated, may hold values from -1.25 to 1.25
- stiff_middle: float32 [27, 27], replicated
- smooth_middle: float32 [27, 27], replicated
- restrict_middle: float32 [8, 27], replicated, may hold values from -1.25 to 1.25
- neighbor: int32 [393216, 6], P(('region', 'group')), may hold values from 0 to 864, as said below
- send_group: int32 [1024, 2, 192], P(('region', 'group')), may hold values from 0 to 383, as said below
- send_region: int32 [1024, 2, 48], P(('region', 'group')), may hold values from 0 to 383, as said below
- ghost_orient: int32 [1024, 480], P(('region', 'group')), may hold values from 0 to 7, as said below
- corners: int32 [393216, 8], P(('region', 'group')), may hold values from 0 to 14624, as said below
Outputs:
- solution: float32 [216, 393216], P(None, ('region', 'group'))
The draws below stay inside these ranges and needn't reach their ends.
Inputs may be any that keep to these rules, and one draw needn't show every extreme that they name: `neighbor`: Device-local slot indices; entries at or above 384 follow the ghost ranges of the steps, matching send_group and send_region of the adjacent devices; 864 marks the box's z ends. `send_group`: Device-local slots; position k is y * 24 + z of the element on that side. `send_region`: Device-local slots; position k is x * 24 + z of the element on that side. `ghost_orient`: positions follow the ghost ranges of neighbor; the two sides of one shared face carry mutually inverse codes. The elements of device (r, g) have corners only on vertex planes g * 2 to (g + 1) * 2 along x.
All inputs are finite; a program needn't handle non-finite values.
Results may differ from the reference program's by a relative error of at most 0.0003.
Values sent between devices are 32-bit elements; how exact they have to be, the bound alone decides.
No kernel may reach another device: no remote copies, remote signals or barrier semaphores. Data moves between devices by JAX's collectives and lax.ppermute only.
A program may use at most 32 MiB of HBM per device.

```python
import math
import jax
import jax.numpy as jnp
import numpy as np
from jax import lax

FINE_PTS = 6
MID_PTS = 3
FINE_NODES = 216
MID_NODES = 27
BX = 2
BY = 8
BZ = 24
ELEMS_DEV = 384
ELEMS = 393216
N_REGION = 32
N_GROUP = 32


def dominant(key, extent, diag_low, diag_high, spread):
    upper_part = jax.random.uniform(jax.random.fold_in(key, 1), (extent, extent), jnp.float32, -1.0, 1.0)
    row_ids = jnp.arange(extent, dtype=jnp.int32)[:, None]
    col_ids = jnp.arange(extent, dtype=jnp.int32)[None, :]
    mirrored = jnp.where(row_ids < col_ids, upper_part, upper_part.T)
    off_part = jnp.where(row_ids == col_ids, 0.0, mirrored) * (spread / extent)
    diagonal = jax.random.uniform(jax.random.fold_in(key, 2), (extent,), jnp.float32, diag_low, diag_high)
    return off_part + jnp.where(row_ids == col_ids, diagonal[:, None], 0.0)


def slot_orders(key):
    devices = N_REGION * N_GROUP
    elements = BX * BY * BZ
    order_key = jax.random.fold_in(key, 101)

    def shuffle(device):
        return jax.random.permutation(jax.random.fold_in(order_key, device), elements).astype(jnp.int32)
    return jax.vmap(shuffle)(jnp.arange(devices, dtype=jnp.int32))


def draw_right_side(key, part):
    own_key = jax.random.fold_in(key, 21)
    shape_all = (FINE_NODES, ELEMS)
    orders = slot_orders(key)
    pos_y = (orders // BZ % BY).astype(jnp.float32)
    pos_z = (orders % BZ).astype(jnp.float32)
    y_mode = max(1, min(3, BY - 1))
    pattern = jnp.sin(y_mode * math.pi / BY * (pos_y + 0.5)) * jnp.sin(math.pi / BZ * (pos_z + 0.5))
    coherent = 2.5 * pattern.reshape(-1)[None, :]
    values = coherent + 0.6 * jax.random.normal(own_key, shape_all, jnp.float32)
    return jnp.clip(values, -4.0, 4.0)


def draw_stiff_fine(key, part):
    return dominant(jax.random.fold_in(key, 11), FINE_NODES, 1.0, 2.0, 1.0)


def draw_smooth_fine(key, part):
    return dominant(jax.random.fold_in(key, 12), FINE_NODES, 0.1, 0.2, 0.1)


def draw_stiff_middle(key, part):
    return dominant(jax.random.fold_in(key, 13), MID_NODES, 1.0, 2.0, 1.0)


def draw_smooth_middle(key, part):
    return dominant(jax.random.fold_in(key, 14), MID_NODES, 0.1, 0.2, 0.1)


def mesh_tables(key):
    devices = N_REGION * N_GROUP
    elements = BX * BY * BZ
    group_faces = BY * BZ
    region_faces = BX * BZ
    ghosts = 2 * group_faces + 2 * region_faces
    vert_x = N_GROUP * BX + 1
    orders = slot_orders(key)
    dev_rows = jnp.arange(devices, dtype=jnp.int32)[:, None]
    slot_table = jnp.zeros((devices, elements), jnp.int32).at[dev_rows, orders].set(jnp.broadcast_to(jnp.arange(elements, dtype=jnp.int32)[None, :], (devices, elements)))
    pos_x = orders // (BY * BZ)
    pos_y = orders // BZ % BY
    pos_z = orders % BZ

    def slot_at(cell_x, cell_y, cell_z):
        linear = (jnp.clip(cell_x, 0, BX - 1) * BY + jnp.clip(cell_y, 0, BY - 1)) * BZ + jnp.clip(cell_z, 0, BZ - 1)
        return jnp.take_along_axis(slot_table, linear, axis=1)
    yz_pos = pos_y * BZ + pos_z
    xz_pos = pos_x * BZ + pos_z
    zero_slot = elements + ghosts
    face_list = [jnp.where(pos_x > 0, slot_at(pos_x - 1, pos_y, pos_z), elements + yz_pos), jnp.where(pos_x < BX - 1, slot_at(pos_x + 1, pos_y, pos_z), elements + group_faces + yz_pos), jnp.where(pos_y > 0, slot_at(pos_x, pos_y - 1, pos_z), elements + 2 * group_faces + xz_pos), jnp.where(pos_y < BY - 1, slot_at(pos_x, pos_y + 1, pos_z), elements + 2 * group_faces + region_faces + xz_pos), jnp.where(pos_z > 0, slot_at(pos_x, pos_y, pos_z - 1), zero_slot), jnp.where(pos_z < BZ - 1, slot_at(pos_x, pos_y, pos_z + 1), zero_slot)]
    neighbor = jnp.stack(face_list, axis=2).reshape(devices * elements, 6).astype(jnp.int32)
    face_ids = jnp.arange(group_faces, dtype=jnp.int32)
    send_group = jnp.stack([slot_table[:, face_ids], slot_table[:, (BX - 1) * BY * BZ + face_ids]], axis=1)
    region_ids = jnp.arange(region_faces, dtype=jnp.int32)
    across_x = region_ids // BZ
    along_z = region_ids % BZ
    send_region = jnp.stack([slot_table[:, across_x * BY * BZ + along_z], slot_table[:, across_x * BY * BZ + (BY - 1) * BZ + along_z]], axis=1)
    group_index = (jnp.arange(devices, dtype=jnp.int32) % N_GROUP)[:, None, None]
    corner_ids = jnp.arange(8, dtype=jnp.int32)
    shift_x = (corner_ids // 4)[None, None, :]
    shift_y = (corner_ids // 2 % 2)[None, None, :]
    shift_z = (corner_ids % 2)[None, None, :]
    vertex_x = group_index * BX + pos_x[:, :, None] + shift_x
    vertex_y = pos_y[:, :, None] + shift_y
    vertex_z = pos_z[:, :, None] + shift_z
    corners = ((vertex_z * (BY + 1) + vertex_y) * vert_x + vertex_x).reshape(devices * elements, 8).astype(jnp.int32)
    codes_x = jax.random.randint(jax.random.fold_in(key, 102), (N_REGION, N_GROUP, group_faces), 0, 8)
    codes_y = jax.random.randint(jax.random.fold_in(key, 103), (N_REGION, N_GROUP, region_faces), 0, 8)
    inverse = jnp.array([0, 3, 2, 1, 4, 5, 6, 7], jnp.int32)
    orient = jnp.concatenate([jnp.roll(codes_x, 1, axis=1), inverse[codes_x], jnp.roll(codes_y, 1, axis=0), inverse[codes_y]], axis=2)
    orient = orient.reshape(devices, ghosts).astype(jnp.int32)
    return (neighbor, send_group, send_region, orient, corners)


def draw_neighbor(key, part):
    return mesh_tables(key)[0]


def draw_send_group(key, part):
    return mesh_tables(key)[1]


def draw_send_region(key, part):
    return mesh_tables(key)[2]


def draw_ghost_orient(key, part):
    return mesh_tables(key)[3]


def draw_corners(key, part):
    return mesh_tables(key)[4]


def normal_values(rng, shape, scale, limit, held_as=jnp.bfloat16):
    values = jax.random.normal(rng, shape, jnp.float32) * scale
    return jnp.minimum(jnp.maximum(values, -limit), limit).astype(held_as)


def setup_inputs(seed: int = 0) -> dict:
    arg_keys = jax.random.split(jax.random.key(seed), 13)
    return {
        "right_side": draw_right_side(jax.random.fold_in(arg_keys[12], 71), 0),
        "stiff_fine": draw_stiff_fine(jax.random.fold_in(arg_keys[12], 71), 0),
        "smooth_fine": draw_smooth_fine(jax.random.fold_in(arg_keys[12], 71), 0),
        "restrict_fine": normal_values(arg_keys[3], (MID_NODES, FINE_NODES), MID_NODES ** -0.5, 1.25, jnp.float32),
        "stiff_middle": draw_stiff_middle(jax.random.fold_in(arg_keys[12], 71), 0),
        "smooth_middle": draw_smooth_middle(jax.random.fold_in(arg_keys[12], 71), 0),
        "restrict_middle": normal_values(arg_keys[6], (8, MID_NODES), MID_NODES ** -0.5, 1.25, jnp.float32),
        "neighbor": draw_neighbor(jax.random.fold_in(arg_keys[12], 71), 0),
        "send_group": draw_send_group(jax.random.fold_in(arg_keys[12], 71), 0),
        "send_region": draw_send_region(jax.random.fold_in(arg_keys[12], 71), 0),
        "ghost_orient": draw_ghost_orient(jax.random.fold_in(arg_keys[12], 71), 0),
        "corners": draw_corners(jax.random.fold_in(arg_keys[12], 71), 0),
    }


HIGHEST = lax.Precision.HIGHEST
penalty_fine = 1.0
penalty_middle = 1.0

def orient_lookup(points):
    lookup = np.zeros((8, points * points), np.int32)
    for code_index in range(8):
        for row_index in range(points):
            for col_index in range(points):
                first_pos, second_pos = (row_index, col_index)
                if code_index >= 4:
                    first_pos, second_pos = (second_pos, first_pos)
                for rotation in range(code_index % 4):
                    first_pos, second_pos = (second_pos, points - 1 - first_pos)
                lookup[code_index, row_index * points + col_index] = first_pos * points + second_pos
    return lookup

def reorient(blocks, code_rows, points):
    stacked = blocks[:, orient_lookup(points)]
    picked = (code_rows[:, None] == jnp.arange(8, dtype=jnp.int32)[None, :, None, None]).astype(jnp.float32)
    return lax.optimization_barrier(jnp.sum(stacked * picked[:, :, None], axis=1))

def face_traces(current, points):
    rest = current.shape[1:]
    blocked = current.reshape((points, points, points) + rest)
    last_node = points - 1
    pieces = [blocked[0], blocked[last_node], blocked[:, 0], blocked[:, last_node], blocked[:, :, 0], blocked[:, :, last_node]]
    return [face_piece.reshape((points * points,) + rest) for face_piece in pieces]

def take_columns(trace_rows, indices):
    return jnp.take_along_axis(trace_rows, indices[None, :, :], axis=2)

def operate(current, stiffness, penalty, points, region_links, group_sends, code_rows, region_ghosts):
    traces = face_traces(current, points)
    group_count = group_sends.shape[2]
    region_count = region_ghosts.shape[3]
    low_send = take_columns(traces[0], group_sends[:, 0])
    high_send = take_columns(traces[1], group_sends[:, 1])
    blank_rows = jnp.zeros_like(low_send[:, :1])
    from_lower = jnp.concatenate([blank_rows, high_send[:, :-1]], axis=1)
    from_upper = jnp.concatenate([low_send[:, 1:], blank_rows], axis=1)
    group_codes = jnp.transpose(code_rows[:, :2 * group_count].reshape(N_GROUP, 2, group_count), (1, 0, 2))
    region_codes = jnp.transpose(code_rows[:, 2 * group_count:].reshape(N_GROUP, 2, region_count), (1, 0, 2))
    oriented_group = reorient(jnp.stack([from_lower, from_upper]), group_codes, points)
    oriented_region = reorient(region_ghosts, region_codes, points)
    ghosts = jnp.concatenate([oriented_group[0], oriented_group[1], oriented_region[0], oriented_region[1]], axis=2)
    plane_size = points * points
    padding = jnp.zeros((plane_size, N_GROUP, 1), jnp.float32)
    product = jnp.einsum('ij,jge->ige', stiffness, current, precision=HIGHEST)
    elements = current.shape[2]
    blocked = product.reshape(points, points, points, N_GROUP, elements)
    jump_terms = []
    for face_index in range(6):
        source = jnp.concatenate([traces[face_index ^ 1], ghosts, padding], axis=2)
        outside = jnp.take_along_axis(source, region_links[:, :, face_index][None], axis=2)
        jump_terms.append((penalty * (traces[face_index] - outside)).reshape(points, points, N_GROUP, elements))
    last_node = points - 1
    blocked = blocked.at[0].add(jump_terms[0])
    blocked = blocked.at[last_node].add(jump_terms[1])
    blocked = blocked.at[:, 0].add(jump_terms[2])
    blocked = blocked.at[:, last_node].add(jump_terms[3])
    blocked = blocked.at[:, :, 0].add(jump_terms[4])
    blocked = blocked.at[:, :, last_node].add(jump_terms[5])
    return blocked.reshape(points * points * points, N_GROUP, elements)

def region_sends(current, points, region_send):
    traces = face_traces(current, points)
    return jnp.stack([take_columns(traces[2], region_send[:, 0]), take_columns(traces[3], region_send[:, 1])])

def ghosts_from(sent_rows):
    blank_rows = jnp.zeros_like(sent_rows[:1, 0])
    from_lower = jnp.concatenate([blank_rows, sent_rows[:-1, 1]], axis=0)
    from_upper = jnp.concatenate([sent_rows[1:, 0], blank_rows], axis=0)
    return jnp.stack([from_lower, from_upper], axis=1)

def sine_basis(extent):
    ordinal = jnp.arange(1, extent + 1, dtype=jnp.int32)
    wrapped = ordinal[:, None] * ordinal[None, :] % (2 * (extent + 1))
    return math.sqrt(2.0 / (extent + 1)) * jnp.sin(wrapped.astype(jnp.float32) * (math.pi / (extent + 1)))

def spectrum(extent):
    cosine = jnp.cos(jnp.arange(1, extent + 1, dtype=jnp.int32).astype(jnp.float32) * (math.pi / (extent + 1)))
    return (2.0 - 2.0 * cosine, (4.0 + 2.0 * cosine) / 6.0)

def transform(volume, basis_z, basis_y, basis_x):
    turned = jnp.einsum('zyx,xk->zyk', volume, basis_x, precision=HIGHEST)
    turned = jnp.einsum('zyk,yj->zjk', turned, basis_y, precision=HIGHEST)
    return jnp.einsum('zjk,zi->ijk', turned, basis_z, precision=HIGHEST)

def coarse_solve(interior):
    depth_count, height_count, breadth_count = interior.shape
    basis_z, basis_y, basis_x = (sine_basis(depth_count), sine_basis(height_count), sine_basis(breadth_count))
    stiff_z, mass_z = spectrum(depth_count)
    stiff_y, mass_y = spectrum(height_count)
    stiff_x, mass_x = spectrum(breadth_count)
    eigen_sum = stiff_z[:, None, None] * mass_y[None, :, None] * mass_x[None, None, :] + mass_z[:, None, None] * stiff_y[None, :, None] * mass_x[None, None, :] + mass_z[:, None, None] * mass_y[None, :, None] * stiff_x[None, None, :]
    return transform(transform(interior, basis_z, basis_y, basis_x) / eigen_sum, basis_z, basis_y, basis_x)

def reference(right_side, stiff_fine, smooth_fine, restrict_fine, stiff_middle, smooth_middle, restrict_middle, neighbor, send_group, send_region, ghost_orient, corners):
    devices = N_REGION * N_GROUP
    vert_x = N_GROUP * BX + 1
    reshaped = right_side.reshape(FINE_NODES, devices, ELEMS_DEV)
    links_all = neighbor.reshape(devices, ELEMS_DEV, 6)
    corners_all = corners.reshape(devices, ELEMS_DEV, 8)

    def device_rows(array, region):
        first_dev = (region * N_GROUP).astype(jnp.int32)
        return lax.dynamic_slice_in_dim(array, first_dev, N_GROUP, 0)

    def region_data(region):
        first_dev = (region * N_GROUP).astype(jnp.int32)
        source = lax.dynamic_slice_in_dim(reshaped, first_dev, N_GROUP, 1)
        return (source, device_rows(links_all, region), device_rows(send_group, region), device_rows(send_region, region), device_rows(ghost_orient, region))

    def pick(array, region):
        return lax.dynamic_index_in_dim(array, region, 0, keepdims=False)

    def smooth_source(source):
        return jnp.einsum('ij,jge->ige', smooth_fine, source, precision=HIGHEST)
    regions = jnp.arange(N_REGION, dtype=jnp.int32)

    def section_one(region):
        source, region_links, group_sends, region_send, code_rows = region_data(region)
        return region_sends(smooth_source(source), FINE_PTS, region_send)
    ghosts_a = ghosts_from(lax.map(section_one, regions))

    def section_two(region):
        source, region_links, group_sends, region_send, code_rows = region_data(region)
        smoothed = smooth_source(source)
        residual = source - operate(smoothed, stiff_fine, penalty_fine, FINE_PTS, region_links, group_sends, code_rows, pick(ghosts_a, region))
        middle_rhs = jnp.einsum('ij,jge->ige', restrict_fine, residual, precision=HIGHEST)
        middle_fix = jnp.einsum('ij,jge->ige', smooth_middle, middle_rhs, precision=HIGHEST)
        return (middle_rhs, middle_fix, region_sends(middle_fix, MID_PTS, region_send))
    rhs_all, fix_all, sent_b = lax.map(section_two, regions)
    ghosts_b = ghosts_from(sent_b)

    def section_three(region):
        source, region_links, group_sends, region_send, code_rows = region_data(region)
        middle_rhs = pick(rhs_all, region)
        middle_fix = pick(fix_all, region)
        middle_res = middle_rhs - operate(middle_fix, stiff_middle, penalty_middle, MID_PTS, region_links, group_sends, code_rows, pick(ghosts_b, region))
        corner_terms = jnp.einsum('ij,jge->ige', restrict_middle, middle_res, precision=HIGHEST)
        corner_ids = jnp.transpose(device_rows(corners_all, region), (2, 0, 1))
        assembled = jnp.zeros(((BZ + 1) * (BY + 1) * vert_x,), jnp.float32).at[corner_ids.reshape(-1)].add(corner_terms.reshape(-1))
        interior = assembled.reshape(BZ + 1, BY + 1, vert_x)[1:BZ, 1:BY, 1:vert_x - 1]
        solved = coarse_solve(interior)
        padded = jnp.pad(solved, ((1, 1), (1, 1), (1, 1))).reshape(-1)
        coarse_fix = padded[corner_ids]
        middle_corr = middle_fix + jnp.einsum('ai,age->ige', restrict_middle, coarse_fix, precision=HIGHEST)
        return (middle_corr, region_sends(middle_corr, MID_PTS, region_send))
    corr_all, sent_c = lax.map(section_three, regions)
    ghosts_c = ghosts_from(sent_c)

    def finish_middle(region, region_links, group_sends, code_rows):
        middle_corr = pick(corr_all, region)
        middle_rhs = pick(rhs_all, region)
        middle_left = middle_rhs - operate(middle_corr, stiff_middle, penalty_middle, MID_PTS, region_links, group_sends, code_rows, pick(ghosts_c, region))
        return middle_corr + jnp.einsum('ij,jge->ige', smooth_middle, middle_left, precision=HIGHEST)

    def section_four(region):
        source, region_links, group_sends, region_send, code_rows = region_data(region)
        middle_post = finish_middle(region, region_links, group_sends, code_rows)
        current = smooth_source(source) + jnp.einsum('ai,age->ige', restrict_fine, middle_post, precision=HIGHEST)
        return (middle_post, region_sends(current, FINE_PTS, region_send))
    post_all, sent_d = lax.map(section_four, regions)
    ghosts_d = ghosts_from(sent_d)

    def section_five(region):
        source, region_links, group_sends, region_send, code_rows = region_data(region)
        middle_post = pick(post_all, region)
        current = smooth_source(source) + jnp.einsum('ai,age->ige', restrict_fine, middle_post, precision=HIGHEST)
        left_over = source - operate(current, stiff_fine, penalty_fine, FINE_PTS, region_links, group_sends, code_rows, pick(ghosts_d, region))
        return current + jnp.einsum('ij,jge->ige', smooth_fine, left_over, precision=HIGHEST)
    outputs = lax.map(section_five, regions)
    return jnp.transpose(outputs, (1, 0, 2, 3)).reshape(FINE_NODES, ELEMS)
```

```python
import math

import jax
import jax.numpy as jnp
import numpy as np
from jax import lax
from jax.sharding import PartitionSpec as P

FINE_PTS = 6
MID_PTS = 3
BX = 2
BY = 8
BZ = 24


HIGHEST = lax.Precision.HIGHEST
penalty_fine = 1.0
penalty_middle = 1.0


def mm(a, b):
    return jnp.dot(a, b, precision=HIGHEST, preferred_element_type=jnp.float32)


def orient_lookup(points):
    lookup = np.zeros((8, points * points), np.int32)
    for code_index in range(8):
        for row_index in range(points):
            for col_index in range(points):
                first_pos, second_pos = (row_index, col_index)
                if code_index >= 4:
                    first_pos, second_pos = (second_pos, first_pos)
                for rotation in range(code_index % 4):
                    first_pos, second_pos = (second_pos, points - 1 - first_pos)
                lookup[code_index, row_index * points + col_index] = first_pos * points + second_pos
    return lookup


def orient_matrix(points):
    lookup = orient_lookup(points)
    plane = points * points
    mat = np.zeros((8 * plane, plane), np.float32)
    for code_index in range(8):
        mat[code_index * plane + np.arange(plane), lookup[code_index]] = 1.0
    return mat


def face_nodes(points):
    ids = np.arange(points**3).reshape(points, points, points)
    last = points - 1
    pieces = [ids[0], ids[last], ids[:, 0], ids[:, last], ids[:, :, 0], ids[:, :, last]]
    return np.stack([p.reshape(-1) for p in pieces])


def trace_matrix(points):
    nodes = face_nodes(points)
    plane = points * points
    mat = np.zeros((6 * plane, points**3), np.float32)
    for face_index in range(6):
        mat[face_index * plane + np.arange(plane), nodes[face_index]] = 1.0
    return mat


def make_tables(neighbor, send_group, send_region, ghost_orient):
    elements = neighbor.shape[0]
    group_count = send_group.shape[2]
    region_count = send_region.shape[2]
    ghosts = 2 * group_count + 2 * region_count
    slots = jnp.arange(elements, dtype=jnp.int32)
    sources = jnp.arange(elements + ghosts, dtype=jnp.int32)
    gather = (neighbor.T[:, None, :] == sources[None, :, None]).astype(jnp.float32)
    pick_group = (send_group[0][:, None, :] == slots[None, :, None]).astype(jnp.float32)
    pick_region = (send_region[0][:, None, :] == slots[None, :, None]).astype(jnp.float32)
    codes = (ghost_orient[0][None, :] == jnp.arange(8, dtype=jnp.int32)[:, None]).astype(
        jnp.float32
    )
    return gather, pick_group, pick_region, codes


def shift(block, axis, step):
    count = lax.axis_size(axis)
    if step > 0:
        pairs = [(i, i + 1) for i in range(count - 1)]
    else:
        pairs = [(i + 1, i) for i in range(count - 1)]
    return lax.ppermute(block, axis, pairs)


def apply_level(current, stiffness, points, tables):
    gather, pick_group, pick_region, codes = tables
    plane = points * points
    cube = points**3
    elements = current.shape[1]
    select = jnp.asarray(trace_matrix(points))
    both = mm(jnp.concatenate([stiffness, select], axis=0), current)
    product = both[:cube]
    traces = both[cube:].reshape(6, plane, elements)
    group_out = jnp.einsum(
        "snj,sjk->snk", traces[0:2], pick_group, precision=HIGHEST,
        preferred_element_type=jnp.float32,
    )
    region_out = jnp.einsum(
        "snj,sjk->snk", traces[2:4], pick_region, precision=HIGHEST,
        preferred_element_type=jnp.float32,
    )
    raw = jnp.concatenate(
        [
            shift(group_out[1], "group", 1),
            shift(group_out[0], "group", -1),
            shift(region_out[1], "region", 1),
            shift(region_out[0], "region", -1),
        ],
        axis=1,
    )
    turned = mm(jnp.asarray(orient_matrix(points)), raw).reshape(8, plane, -1)
    ghosts = jnp.sum(turned * codes[:, None, :], axis=0)
    swapped = traces[np.array([1, 0, 3, 2, 5, 4])]
    source = jnp.concatenate(
        [swapped, jnp.broadcast_to(ghosts[None], (6,) + ghosts.shape)], axis=2
    )
    outside = jnp.einsum(
        "fnq,fqe->fne", source, gather, precision=HIGHEST, preferred_element_type=jnp.float32
    )
    jumps = (traces - outside).reshape(6 * plane, elements)
    return product + mm(select.T, jumps)


def sine_basis(extent):
    ordinal = jnp.arange(1, extent + 1, dtype=jnp.int32)
    wrapped = ordinal[:, None] * ordinal[None, :] % (2 * (extent + 1))
    return math.sqrt(2.0 / (extent + 1)) * jnp.sin(
        wrapped.astype(jnp.float32) * (math.pi / (extent + 1))
    )


def spectrum(extent):
    cosine = jnp.cos(
        jnp.arange(1, extent + 1, dtype=jnp.int32).astype(jnp.float32) * (math.pi / (extent + 1))
    )
    return (2.0 - 2.0 * cosine, (4.0 + 2.0 * cosine) / 6.0)


def transform(volume, basis_z, basis_y, basis_x):
    turned = jnp.einsum("zyx,xk->zyk", volume, basis_x, precision=HIGHEST)
    turned = jnp.einsum("zyk,yj->zjk", turned, basis_y, precision=HIGHEST)
    return jnp.einsum("zjk,zi->ijk", turned, basis_z, precision=HIGHEST)


def coarse_solve(interior):
    depth_count, height_count, breadth_count = interior.shape
    basis_z, basis_y, basis_x = (
        sine_basis(depth_count),
        sine_basis(height_count),
        sine_basis(breadth_count),
    )
    stiff_z, mass_z = spectrum(depth_count)
    stiff_y, mass_y = spectrum(height_count)
    stiff_x, mass_x = spectrum(breadth_count)
    eigen_sum = (
        stiff_z[:, None, None] * mass_y[None, :, None] * mass_x[None, None, :]
        + mass_z[:, None, None] * stiff_y[None, :, None] * mass_x[None, None, :]
        + mass_z[:, None, None] * mass_y[None, :, None] * stiff_x[None, None, :]
    )
    return transform(
        transform(interior, basis_z, basis_y, basis_x) / eigen_sum, basis_z, basis_y, basis_x
    )


def gather_slab(local, width):
    count = local.shape[0]
    index = lax.axis_index("group")
    full = lax.dynamic_update_slice(
        jnp.zeros((count, BX * width + 1), jnp.float32), local, (0, BX * index)
    )
    for bit in range(int(math.log2(width))):
        partner = [(i, i ^ (1 << bit)) for i in range(width)]
        full = full + lax.ppermute(full, "group", partner)
    return full


def body(
    right_side,
    stiff_fine,
    smooth_fine,
    restrict_fine,
    stiff_middle,
    smooth_middle,
    restrict_middle,
    neighbor,
    send_group,
    send_region,
    ghost_orient,
    corners,
):
    tables = make_tables(neighbor, send_group, send_region, ghost_orient)
    smoothed = mm(smooth_fine, right_side)
    residual = right_side - apply_level(smoothed, stiff_fine, FINE_PTS, tables)
    middle_rhs = mm(restrict_fine, residual)
    middle_fix = mm(smooth_middle, middle_rhs)
    middle_res = middle_rhs - apply_level(middle_fix, stiff_middle, MID_PTS, tables)
    corner_terms = mm(restrict_middle, middle_res)

    width_group = lax.axis_size("group")
    vert_x = width_group * BX + 1
    planes = (BZ + 1) * (BY + 1)
    corner_ids = corners.T.reshape(-1)
    plane_ids = corner_ids // vert_x
    column = corner_ids - plane_ids * vert_x - BX * lax.axis_index("group")
    on_plane = (plane_ids[None, :] == jnp.arange(planes, dtype=jnp.int32)[:, None]).astype(
        jnp.float32
    )
    on_column = (column[:, None] == jnp.arange(BX + 1, dtype=jnp.int32)[None, :]).astype(
        jnp.float32
    )
    local = mm(on_plane, corner_terms.reshape(-1)[:, None] * on_column)
    assembled = gather_slab(local, width_group)
    interior = assembled.reshape(BZ + 1, BY + 1, vert_x)[1:BZ, 1:BY, 1 : vert_x - 1]
    solved = coarse_solve(interior)
    padded = jnp.pad(solved, ((1, 1), (1, 1), (1, 1)))
    mine = lax.dynamic_slice_in_dim(padded, BX * lax.axis_index("group"), BX + 1, axis=2)
    picked = mm(mine.reshape(planes, BX + 1).T, on_plane)
    coarse_fix = jnp.sum(picked * on_column.T, axis=0).reshape(corners.shape[1], -1)

    middle_corr = middle_fix + mm(restrict_middle.T, coarse_fix)
    middle_left = middle_rhs - apply_level(middle_corr, stiff_middle, MID_PTS, tables)
    middle_post = middle_corr + mm(smooth_middle, middle_left)
    current = smoothed + mm(restrict_fine.T, middle_post)
    left_over = right_side - apply_level(current, stiff_fine, FINE_PTS, tables)
    return current + mm(smooth_fine, left_over)


def solution(mesh):
    return jax.shard_map(
        body,
        mesh=mesh,
        in_specs=(
            P(None, ("region", "group")),
            P(),
            P(),
            P(),
            P(),
            P(),
            P(),
            P(("region", "group"), None),
            P(("region", "group"), None, None),
            P(("region", "group"), None, None),
            P(("region", "group"), None),
            P(("region", "group"), None),
        ),
        out_specs=P(None, ("region", "group")),
        check_vma=False,
    )
```

```python
import math

import jax
import jax.numpy as jnp
import numpy as np
from jax import lax
from jax.sharding import PartitionSpec as P

FINE_PTS = 6
MID_PTS = 3
BX = 2
BY = 8
BZ = 24


HIGHEST = lax.Precision.HIGHEST
penalty_fine = 1.0
penalty_middle = 1.0


def mm(a, b):
    return jnp.dot(a, b, precision=HIGHEST, preferred_element_type=jnp.float32)


def orient_lookup(points):
    lookup = np.zeros((8, points * points), np.int32)
    for code_index in range(8):
        for row_index in range(points):
            for col_index in range(points):
                first_pos, second_pos = (row_index, col_index)
                if code_index >= 4:
                    first_pos, second_pos = (second_pos, first_pos)
                for rotation in range(code_index % 4):
                    first_pos, second_pos = (second_pos, points - 1 - first_pos)
                lookup[code_index, row_index * points + col_index] = first_pos * points + second_pos
    return lookup


def orient_matrix(points):
    lookup = orient_lookup(points)
    plane = points * points
    mat = np.zeros((8 * plane, plane), np.float32)
    for code_index in range(8):
        mat[code_index * plane + np.arange(plane), lookup[code_index]] = 1.0
    return mat


def face_nodes(points):
    ids = np.arange(points**3).reshape(points, points, points)
    last = points - 1
    pieces = [ids[0], ids[last], ids[:, 0], ids[:, last], ids[:, :, 0], ids[:, :, last]]
    return np.stack([p.reshape(-1) for p in pieces])


def trace_matrix(points):
    nodes = face_nodes(points)
    plane = points * points
    mat = np.zeros((6 * plane, points**3), np.float32)
    for face_index in range(6):
        mat[face_index * plane + np.arange(plane), nodes[face_index]] = 1.0
    return mat


def make_tables(neighbor, send_group, send_region, ghost_orient):
    elements = neighbor.shape[0]
    group_count = send_group.shape[2]
    region_count = send_region.shape[2]
    ghosts = 2 * group_count + 2 * region_count
    slots = jnp.arange(elements, dtype=jnp.int32)
    sources = jnp.arange(elements + ghosts, dtype=jnp.int32)
    gather = (neighbor.T[:, None, :] == sources[None, :, None]).astype(jnp.bfloat16)
    pick_group = (send_group[0][:, None, :] == slots[None, :, None]).astype(jnp.float32)
    pick_region = (send_region[0][:, None, :] == slots[None, :, None]).astype(jnp.float32)
    codes = (ghost_orient[0][None, :] == jnp.arange(8, dtype=jnp.int32)[:, None]).astype(
        jnp.float32
    )
    return gather, pick_group, pick_region, codes


def shift(block, axis, step):
    count = lax.axis_size(axis)
    if step > 0:
        pairs = [(i, i + 1) for i in range(count - 1)]
    else:
        pairs = [(i + 1, i) for i in range(count - 1)]
    return lax.ppermute(block, axis, pairs)


def apply_level(current, stiffness, points, tables):
    gather, pick_group, pick_region, codes = tables
    plane = points * points
    cube = points**3
    elements = current.shape[1]
    select = jnp.asarray(trace_matrix(points))
    both = mm(jnp.concatenate([stiffness, select], axis=0), current)
    product = both[:cube]
    traces = both[cube:].reshape(6, plane, elements)
    group_out = jnp.einsum(
        "snj,sjk->snk", traces[0:2], pick_group, precision=HIGHEST,
        preferred_element_type=jnp.float32,
    )
    region_out = jnp.einsum(
        "snj,sjk->snk", traces[2:4], pick_region, precision=HIGHEST,
        preferred_element_type=jnp.float32,
    )
    from_region_low = shift(region_out[1], "region", 1)
    from_region_high = shift(region_out[0], "region", -1)
    from_group_low = shift(group_out[1], "group", 1)
    from_group_high = shift(group_out[0], "group", -1)
    raw = jnp.concatenate(
        [from_group_low, from_group_high, from_region_low, from_region_high], axis=1
    )
    turned = mm(jnp.asarray(orient_matrix(points)), raw).reshape(8, plane, -1)
    ghosts = jnp.sum(turned * codes[:, None, :], axis=0)
    swapped = traces[np.array([1, 0, 3, 2, 5, 4])]
    source = jnp.concatenate(
        [swapped, jnp.broadcast_to(ghosts[None], (6,) + ghosts.shape)], axis=2
    )
    outside = jnp.einsum(
        "fnq,fqe->fne", source, gather.astype(jnp.float32), precision=HIGHEST,
        preferred_element_type=jnp.float32,
    )
    jumps = (traces - outside).reshape(6 * plane, elements)
    return product + mm(select.T, jumps)


def sine_basis(extent):
    ordinal = jnp.arange(1, extent + 1, dtype=jnp.int32)
    wrapped = ordinal[:, None] * ordinal[None, :] % (2 * (extent + 1))
    return math.sqrt(2.0 / (extent + 1)) * jnp.sin(
        wrapped.astype(jnp.float32) * (math.pi / (extent + 1))
    )


def spectrum(extent):
    cosine = jnp.cos(
        jnp.arange(1, extent + 1, dtype=jnp.int32).astype(jnp.float32) * (math.pi / (extent + 1))
    )
    return (2.0 - 2.0 * cosine, (4.0 + 2.0 * cosine) / 6.0)


def transform(volume, basis_z, basis_y, basis_x):
    turned = jnp.einsum("zyx,xk->zyk", volume, basis_x, precision=HIGHEST)
    turned = jnp.einsum("zyk,yj->zjk", turned, basis_y, precision=HIGHEST)
    return jnp.einsum("zjk,zi->ijk", turned, basis_z, precision=HIGHEST)


def coarse_solve(interior):
    depth_count, height_count, breadth_count = interior.shape
    basis_z, basis_y, basis_x = (
        sine_basis(depth_count),
        sine_basis(height_count),
        sine_basis(breadth_count),
    )
    stiff_z, mass_z = spectrum(depth_count)
    stiff_y, mass_y = spectrum(height_count)
    stiff_x, mass_x = spectrum(breadth_count)
    eigen_sum = (
        stiff_z[:, None, None] * mass_y[None, :, None] * mass_x[None, None, :]
        + mass_z[:, None, None] * stiff_y[None, :, None] * mass_x[None, None, :]
        + mass_z[:, None, None] * mass_y[None, :, None] * stiff_x[None, None, :]
    )
    return transform(
        transform(interior, basis_z, basis_y, basis_x) / eigen_sum, basis_z, basis_y, basis_x
    )


def gather_slab(local, width):
    index = lax.axis_index("group")
    vert_x = BX * width + 1
    full = lax.dynamic_update_slice(
        jnp.zeros((local.shape[0], vert_x), jnp.float32), local, (0, BX * index)
    )
    interior = full.reshape(BZ + 1, BY + 1, vert_x)[1:BZ, 1:BY, 1 : vert_x - 1]
    for bit in range(int(math.log2(width))):
        partner = [(i, i ^ (1 << bit)) for i in range(width)]
        interior = interior + lax.ppermute(interior, "group", partner)
    return interior


def body(
    right_side,
    stiff_fine,
    smooth_fine,
    restrict_fine,
    stiff_middle,
    smooth_middle,
    restrict_middle,
    neighbor,
    send_group,
    send_region,
    ghost_orient,
    corners,
):
    tables = make_tables(neighbor, send_group, send_region, ghost_orient)
    smoothed = mm(smooth_fine, right_side)
    residual = right_side - apply_level(smoothed, stiff_fine, FINE_PTS, tables)
    middle_rhs = mm(restrict_fine, residual)
    middle_fix = mm(smooth_middle, middle_rhs)
    middle_res = middle_rhs - apply_level(middle_fix, stiff_middle, MID_PTS, tables)
    corner_terms = mm(restrict_middle, middle_res)

    width_group = lax.axis_size("group")
    vert_x = width_group * BX + 1
    planes = (BZ + 1) * (BY + 1)
    corner_ids = corners.T.reshape(-1)
    plane_ids = corner_ids // vert_x
    column = corner_ids - plane_ids * vert_x - BX * lax.axis_index("group")
    on_plane = (plane_ids[None, :] == jnp.arange(planes, dtype=jnp.int32)[:, None]).astype(
        jnp.bfloat16
    ).astype(jnp.float32)
    on_column = (column[:, None] == jnp.arange(BX + 1, dtype=jnp.int32)[None, :]).astype(
        jnp.float32
    )
    local = mm(on_plane, corner_terms.reshape(-1)[:, None] * on_column)
    interior = gather_slab(local, width_group)
    solved = coarse_solve(interior)
    padded = jnp.pad(solved, ((1, 1), (1, 1), (1, 1)))
    mine = lax.dynamic_slice_in_dim(padded, BX * lax.axis_index("group"), BX + 1, axis=2)
    picked = mm(mine.reshape(planes, BX + 1).T, on_plane)
    coarse_fix = jnp.sum(picked * on_column.T, axis=0).reshape(corners.shape[1], -1)

    middle_corr = middle_fix + mm(restrict_middle.T, coarse_fix)
    middle_left = middle_rhs - apply_level(middle_corr, stiff_middle, MID_PTS, tables)
    middle_post = middle_corr + mm(smooth_middle, middle_left)
    current = smoothed + mm(restrict_fine.T, middle_post)
    left_over = right_side - apply_level(current, stiff_fine, FINE_PTS, tables)
    return current + mm(smooth_fine, left_over)


def solution(mesh):
    return jax.shard_map(
        body,
        mesh=mesh,
        in_specs=(
            P(None, ("region", "group")),
            P(),
            P(),
            P(),
            P(),
            P(),
            P(),
            P(("region", "group"), None),
            P(("region", "group"), None, None),
            P(("region", "group"), None, None),
            P(("region", "group"), None),
            P(("region", "group"), None),
        ),
        out_specs=P(None, ("region", "group")),
        check_vma=False,
    )
```

```python
import math

import jax
import jax.numpy as jnp
import numpy as np
from jax import lax
from jax.sharding import PartitionSpec as P

FINE_PTS = 6
MID_PTS = 3
BX = 2
BY = 8
BZ = 24


HIGHEST = lax.Precision.HIGHEST
penalty_fine = 1.0
penalty_middle = 1.0


def mm(a, b):
    return jnp.dot(a, b, precision=HIGHEST, preferred_element_type=jnp.float32)


def orient_lookup(points):
    lookup = np.zeros((8, points * points), np.int32)
    for code_index in range(8):
        for row_index in range(points):
            for col_index in range(points):
                first_pos, second_pos = (row_index, col_index)
                if code_index >= 4:
                    first_pos, second_pos = (second_pos, first_pos)
                for rotation in range(code_index % 4):
                    first_pos, second_pos = (second_pos, points - 1 - first_pos)
                lookup[code_index, row_index * points + col_index] = first_pos * points + second_pos
    return lookup


def orient_matrix(points):
    lookup = orient_lookup(points)
    plane = points * points
    mat = np.zeros((8 * plane, plane), np.float32)
    for code_index in range(8):
        mat[code_index * plane + np.arange(plane), lookup[code_index]] = 1.0
    return mat


def face_nodes(points):
    ids = np.arange(points**3).reshape(points, points, points)
    last = points - 1
    pieces = [ids[0], ids[last], ids[:, 0], ids[:, last], ids[:, :, 0], ids[:, :, last]]
    return np.stack([p.reshape(-1) for p in pieces])


def trace_matrix(points):
    nodes = face_nodes(points)
    plane = points * points
    mat = np.zeros((6 * plane, points**3), np.float32)
    for face_index in range(6):
        mat[face_index * plane + np.arange(plane), nodes[face_index]] = 1.0
    return mat


def make_tables(neighbor, send_group, send_region, ghost_orient):
    elements = neighbor.shape[0]
    group_count = send_group.shape[2]
    region_count = send_region.shape[2]
    ghosts = 2 * group_count + 2 * region_count
    slots = jnp.arange(elements, dtype=jnp.int32)
    sources = jnp.arange(elements + ghosts, dtype=jnp.int32)
    gather = (neighbor.T[:, None, :] == sources[None, :, None]).astype(jnp.bfloat16)
    pick_group = (send_group[0][:, None, :] == slots[None, :, None]).astype(jnp.float32)
    pick_region = (send_region[0][:, None, :] == slots[None, :, None]).astype(jnp.float32)
    codes = (ghost_orient[0][None, :] == jnp.arange(8, dtype=jnp.int32)[:, None]).astype(
        jnp.float32
    )
    return gather, pick_group, pick_region, codes


def shift(block, axis, step):
    count = lax.axis_size(axis)
    if step > 0:
        pairs = [(i, i + 1) for i in range(count - 1)]
    else:
        pairs = [(i + 1, i) for i in range(count - 1)]
    return lax.ppermute(block, axis, pairs)


def apply_level(current, stiffness, points, tables, extra=None, group_ghosts=None):
    gather, pick_group, pick_region, codes = tables
    plane = points * points
    cube = points**3
    elements = current.shape[1]
    select = jnp.asarray(trace_matrix(points))
    both = mm(jnp.concatenate([stiffness, select], axis=0), current)
    product = both[:cube]
    traces = both[cube:].reshape(6, plane, elements)
    region_out = jnp.einsum(
        "snj,sjk->snk", traces[2:4], pick_region, precision=HIGHEST,
        preferred_element_type=jnp.float32,
    )
    from_region_low = shift(region_out[1], "region", 1)
    from_region_high = shift(region_out[0], "region", -1)
    received = None
    if group_ghosts is None:
        group_out = jnp.einsum(
            "snj,sjk->snk", traces[0:2], pick_group, precision=HIGHEST,
            preferred_element_type=jnp.float32,
        )
        if extra is not None:
            group_out = jnp.concatenate([group_out, extra], axis=1)
        from_group_low = shift(group_out[1], "group", 1)
        from_group_high = shift(group_out[0], "group", -1)
        received = (from_group_low[plane:], from_group_high[plane:])
        group_ghosts = (from_group_low[:plane], from_group_high[:plane])
    raw = jnp.concatenate(
        [group_ghosts[0], group_ghosts[1], from_region_low, from_region_high], axis=1
    )
    turned = mm(jnp.asarray(orient_matrix(points)), raw).reshape(8, plane, -1)
    ghosts = jnp.sum(turned * codes[:, None, :], axis=0)
    swapped = traces[np.array([1, 0, 3, 2, 5, 4])]
    source = jnp.concatenate(
        [swapped, jnp.broadcast_to(ghosts[None], (6,) + ghosts.shape)], axis=2
    )
    outside = jnp.einsum(
        "fnq,fqe->fne", source, gather.astype(jnp.float32), precision=HIGHEST,
        preferred_element_type=jnp.float32,
    )
    jumps = (traces - outside).reshape(6 * plane, elements)
    return product + mm(select.T, jumps), received


def corner_values(window, ids, first_column, planes, vert_x):
    flat = ids.reshape(-1)
    plane_ids = flat // vert_x
    column = flat - plane_ids * vert_x - first_column
    on_plane = (plane_ids[None, :] == jnp.arange(planes, dtype=jnp.int32)[:, None]).astype(
        jnp.float32
    )
    on_column = (
        column[:, None] == jnp.arange(window.shape[1], dtype=jnp.int32)[None, :]
    ).astype(jnp.float32)
    picked = mm(window.T, on_plane)
    return jnp.sum(picked * on_column.T, axis=0).reshape(ids.shape)


def sine_basis(extent):
    ordinal = jnp.arange(1, extent + 1, dtype=jnp.int32)
    wrapped = ordinal[:, None] * ordinal[None, :] % (2 * (extent + 1))
    return math.sqrt(2.0 / (extent + 1)) * jnp.sin(
        wrapped.astype(jnp.float32) * (math.pi / (extent + 1))
    )


def spectrum(extent):
    cosine = jnp.cos(
        jnp.arange(1, extent + 1, dtype=jnp.int32).astype(jnp.float32) * (math.pi / (extent + 1))
    )
    return (2.0 - 2.0 * cosine, (4.0 + 2.0 * cosine) / 6.0)


def transform(volume, basis_z, basis_y, basis_x):
    turned = jnp.einsum("zyx,xk->zyk", volume, basis_x, precision=HIGHEST)
    turned = jnp.einsum("zyk,yj->zjk", turned, basis_y, precision=HIGHEST)
    return jnp.einsum("zjk,zi->ijk", turned, basis_z, precision=HIGHEST)


def coarse_solve(interior):
    depth_count, height_count, breadth_count = interior.shape
    basis_z, basis_y, basis_x = (
        sine_basis(depth_count),
        sine_basis(height_count),
        sine_basis(breadth_count),
    )
    stiff_z, mass_z = spectrum(depth_count)
    stiff_y, mass_y = spectrum(height_count)
    stiff_x, mass_x = spectrum(breadth_count)
    eigen_sum = (
        stiff_z[:, None, None] * mass_y[None, :, None] * mass_x[None, None, :]
        + mass_z[:, None, None] * stiff_y[None, :, None] * mass_x[None, None, :]
        + mass_z[:, None, None] * mass_y[None, :, None] * stiff_x[None, None, :]
    )
    return transform(
        transform(interior, basis_z, basis_y, basis_x) / eigen_sum, basis_z, basis_y, basis_x
    )


def gather_slab(local, width):
    index = lax.axis_index("group")
    vert_x = BX * width + 1
    full = lax.dynamic_update_slice(
        jnp.zeros((local.shape[0], vert_x), jnp.float32), local, (0, BX * index)
    )
    interior = full.reshape(BZ + 1, BY + 1, vert_x)[1:BZ, 1:BY, 1 : vert_x - 1]
    for bit in range(int(math.log2(width))):
        partner = [(i, i ^ (1 << bit)) for i in range(width)]
        interior = interior + lax.ppermute(interior, "group", partner)
    return interior


def body(
    right_side,
    stiff_fine,
    smooth_fine,
    restrict_fine,
    stiff_middle,
    smooth_middle,
    restrict_middle,
    neighbor,
    send_group,
    send_region,
    ghost_orient,
    corners,
):
    tables = make_tables(neighbor, send_group, send_region, ghost_orient)
    width_group = lax.axis_size("group")
    index = lax.axis_index("group")
    vert_x = width_group * BX + 1
    planes = (BZ + 1) * (BY + 1)
    corner_ids = corners.T
    sent_ids = jnp.einsum(
        "nj,sjk->snk", corner_ids.astype(jnp.float32), tables[1], precision=HIGHEST,
        preferred_element_type=jnp.float32,
    )

    smoothed = mm(smooth_fine, right_side)
    operated, received = apply_level(smoothed, stiff_fine, FINE_PTS, tables, extra=sent_ids)
    residual = right_side - operated
    neighbor_ids = jnp.round(jnp.concatenate(received, axis=1)).astype(jnp.int32)
    middle_rhs = mm(restrict_fine, residual)
    middle_fix = mm(smooth_middle, middle_rhs)
    middle_res = middle_rhs - apply_level(middle_fix, stiff_middle, MID_PTS, tables)[0]
    corner_terms = mm(restrict_middle, middle_res)

    plane_ids = corner_ids.reshape(-1) // vert_x
    column = corner_ids.reshape(-1) - plane_ids * vert_x - BX * index
    on_plane = (plane_ids[None, :] == jnp.arange(planes, dtype=jnp.int32)[:, None]).astype(
        jnp.float32
    )
    on_column = (column[:, None] == jnp.arange(BX + 1, dtype=jnp.int32)[None, :]).astype(
        jnp.float32
    )
    local = mm(on_plane, corner_terms.reshape(-1)[:, None] * on_column)
    interior = gather_slab(local, width_group)
    solved = coarse_solve(interior)
    padded = jnp.pad(solved, ((1, 1), (1, 1), (1 + BX, 1 + BX)))
    window = lax.dynamic_slice_in_dim(padded, BX * index, 3 * BX + 1, axis=2)
    window = window.reshape(planes, 3 * BX + 1)
    mine = window[:, BX : 2 * BX + 1]
    coarse_fix = corner_values(mine, corner_ids, BX * index, planes, vert_x)
    neighbor_fix = corner_values(window, neighbor_ids, BX * (index - 1), planes, vert_x)
    face_select = trace_matrix(MID_PTS).reshape(6, MID_PTS**2, MID_PTS**3)
    neighbor_corr = mm(restrict_middle.T, neighbor_fix)
    count = send_group.shape[2]
    low_valid = (index > 0).astype(jnp.float32)
    high_valid = (index < width_group - 1).astype(jnp.float32)
    group_ghosts = (
        mm(jnp.asarray(face_select[1]), neighbor_corr[:, :count]) * low_valid,
        mm(jnp.asarray(face_select[0]), neighbor_corr[:, count:]) * high_valid,
    )

    correction = mm(restrict_middle.T, coarse_fix)
    middle_corr = middle_fix + correction
    middle_left = middle_res - apply_level(
        correction, stiff_middle, MID_PTS, tables, group_ghosts=group_ghosts
    )[0]
    middle_post = middle_corr + mm(smooth_middle, middle_left)
    current = smoothed + mm(restrict_fine.T, middle_post)
    left_over = right_side - apply_level(current, stiff_fine, FINE_PTS, tables)[0]
    return current + mm(smooth_fine, left_over)


def solution(mesh):
    return jax.shard_map(
        body,
        mesh=mesh,
        in_specs=(
            P(None, ("region", "group")),
            P(),
            P(),
            P(),
            P(),
            P(),
            P(),
            P(("region", "group"), None),
            P(("region", "group"), None, None),
            P(("region", "group"), None, None),
            P(("region", "group"), None),
            P(("region", "group"), None),
        ),
        out_specs=P(None, ("region", "group")),
        check_vma=False,
    )
```

```python
import math

import jax
import jax.numpy as jnp
import numpy as np
from jax import lax
from jax.sharding import PartitionSpec as P

FINE_PTS = 6
MID_PTS = 3
BX = 2
BY = 8
BZ = 24


HIGHEST = lax.Precision.HIGHEST
penalty_fine = 1.0
penalty_middle = 1.0


def mm(a, b):
    return jnp.dot(a, b, precision=HIGHEST, preferred_element_type=jnp.float32)


def orient_lookup(points):
    lookup = np.zeros((8, points * points), np.int32)
    for code_index in range(8):
        for row_index in range(points):
            for col_index in range(points):
                first_pos, second_pos = (row_index, col_index)
                if code_index >= 4:
                    first_pos, second_pos = (second_pos, first_pos)
                for rotation in range(code_index % 4):
                    first_pos, second_pos = (second_pos, points - 1 - first_pos)
                lookup[code_index, row_index * points + col_index] = first_pos * points + second_pos
    return lookup


def orient_matrix(points):
    lookup = orient_lookup(points)
    plane = points * points
    mat = np.zeros((8 * plane, plane), np.float32)
    for code_index in range(8):
        mat[code_index * plane + np.arange(plane), lookup[code_index]] = 1.0
    return mat


def face_nodes(points):
    ids = np.arange(points**3).reshape(points, points, points)
    last = points - 1
    pieces = [ids[0], ids[last], ids[:, 0], ids[:, last], ids[:, :, 0], ids[:, :, last]]
    return np.stack([p.reshape(-1) for p in pieces])


def trace_matrix(points):
    nodes = face_nodes(points)
    plane = points * points
    mat = np.zeros((6 * plane, points**3), np.float32)
    for face_index in range(6):
        mat[face_index * plane + np.arange(plane), nodes[face_index]] = 1.0
    return mat


def make_tables(neighbor, send_group, send_region, ghost_orient):
    elements = neighbor.shape[0]
    group_count = send_group.shape[2]
    region_count = send_region.shape[2]
    ghosts = 2 * group_count + 2 * region_count
    slots = jnp.arange(elements, dtype=jnp.int32)
    sources = jnp.arange(elements + ghosts, dtype=jnp.int32)
    gather = (neighbor.T[:, None, :] == sources[None, :, None]).astype(jnp.bfloat16)
    pick_group = (send_group[0][:, None, :] == slots[None, :, None]).astype(jnp.float32)
    pick_region = (send_region[0][:, None, :] == slots[None, :, None]).astype(jnp.float32)
    codes = (ghost_orient[0][None, :] == jnp.arange(8, dtype=jnp.int32)[:, None]).astype(
        jnp.float32
    )
    return gather, pick_group, pick_region, codes


def shift(block, axis, step):
    count = lax.axis_size(axis)
    if step > 0:
        pairs = [(i, i + 1) for i in range(count - 1)]
    else:
        pairs = [(i + 1, i) for i in range(count - 1)]
    return lax.ppermute(block, axis, pairs)


def apply_level(current, stiffness, points, tables, extra=None, group_ghosts=None):
    gather, pick_group, pick_region, codes = tables
    plane = points * points
    cube = points**3
    elements = current.shape[1]
    select = jnp.asarray(trace_matrix(points))
    both = mm(jnp.concatenate([stiffness, select], axis=0), current)
    product = both[:cube]
    traces = both[cube:].reshape(6, plane, elements)
    region_out = jnp.einsum(
        "snj,sjk->snk", traces[2:4], pick_region, precision=HIGHEST,
        preferred_element_type=jnp.float32,
    )
    from_region_low = shift(region_out[1], "region", 1)
    from_region_high = shift(region_out[0], "region", -1)
    received = None
    if group_ghosts is None:
        group_out = jnp.einsum(
            "snj,sjk->snk", traces[0:2], pick_group, precision=HIGHEST,
            preferred_element_type=jnp.float32,
        )
        if extra is not None:
            group_out = jnp.concatenate([group_out, extra], axis=1)
        from_group_low = shift(group_out[1], "group", 1)
        from_group_high = shift(group_out[0], "group", -1)
        received = (from_group_low[plane:], from_group_high[plane:])
        group_ghosts = (from_group_low[:plane], from_group_high[:plane])
    raw = jnp.concatenate(
        [group_ghosts[0], group_ghosts[1], from_region_low, from_region_high], axis=1
    )
    turned = mm(jnp.asarray(orient_matrix(points)), raw).reshape(8, plane, -1)
    ghosts = jnp.sum(turned * codes[:, None, :], axis=0)
    swapped = traces[np.array([1, 0, 3, 2, 5, 4])]
    source = jnp.concatenate(
        [swapped, jnp.broadcast_to(ghosts[None], (6,) + ghosts.shape)], axis=2
    )
    outside = exact_select("fnq,fqe->fne", source, gather, axis=1)
    jumps = (traces - outside).reshape(6 * plane, elements)
    return product + mm(select.T, jumps), received


def exact_select(spec, values, picks, axis):
    high = lax.reduce_precision(values, exponent_bits=8, mantissa_bits=7)
    rest = values - high
    middle = lax.reduce_precision(rest, exponent_bits=8, mantissa_bits=7)
    low = rest - middle
    parts = jnp.concatenate([high, middle, low], axis=axis).astype(jnp.bfloat16)
    out = jnp.einsum(spec, parts, picks, preferred_element_type=jnp.float32)
    size = values.shape[axis]
    first = lax.slice_in_dim(out, 0, size, axis=axis)
    second = lax.slice_in_dim(out, size, 2 * size, axis=axis)
    third = lax.slice_in_dim(out, 2 * size, 3 * size, axis=axis)
    return first + second + third


def corner_values(window, ids, first_column, planes, vert_x):
    flat = ids.reshape(-1)
    plane_ids = flat // vert_x
    column = flat - plane_ids * vert_x - first_column
    on_plane = (plane_ids[None, :] == jnp.arange(planes, dtype=jnp.int32)[:, None]).astype(
        jnp.float32
    )
    on_column = (
        column[:, None] == jnp.arange(window.shape[1], dtype=jnp.int32)[None, :]
    ).astype(jnp.float32)
    picked = mm(window.T, on_plane)
    return jnp.sum(picked * on_column.T, axis=0).reshape(ids.shape)


def sine_basis(extent):
    ordinal = jnp.arange(1, extent + 1, dtype=jnp.int32)
    wrapped = ordinal[:, None] * ordinal[None, :] % (2 * (extent + 1))
    return math.sqrt(2.0 / (extent + 1)) * jnp.sin(
        wrapped.astype(jnp.float32) * (math.pi / (extent + 1))
    )


def spectrum(extent):
    cosine = jnp.cos(
        jnp.arange(1, extent + 1, dtype=jnp.int32).astype(jnp.float32) * (math.pi / (extent + 1))
    )
    return (2.0 - 2.0 * cosine, (4.0 + 2.0 * cosine) / 6.0)


def coarse_solve(interior):
    depth_count, height_count, breadth_count = interior.shape
    basis_z, basis_y, basis_x = (
        sine_basis(depth_count),
        sine_basis(height_count),
        sine_basis(breadth_count),
    )
    stiff_z, mass_z = spectrum(depth_count)
    stiff_y, mass_y = spectrum(height_count)
    stiff_x, mass_x = spectrum(breadth_count)
    eigen_sum = (
        stiff_z[:, None, None] * mass_y[None, :, None] * mass_x[None, None, :]
        + mass_z[:, None, None] * stiff_y[None, :, None] * mass_x[None, None, :]
        + mass_z[:, None, None] * mass_y[None, :, None] * stiff_x[None, None, :]
    ).reshape(depth_count * height_count, breadth_count)
    basis_zy = (basis_z[:, None, :, None] * basis_y[None, :, None, :]).reshape(
        depth_count * height_count, depth_count * height_count
    )
    volume = interior.reshape(depth_count * height_count, breadth_count)
    spectral = mm(basis_zy.T, mm(volume, basis_x)) / eigen_sum
    return mm(basis_zy.T, mm(spectral, basis_x)).reshape(interior.shape)


def gather_slab(local, width):
    index = lax.axis_index("group")
    vert_x = BX * width + 1
    full = lax.dynamic_update_slice(
        jnp.zeros((local.shape[0], vert_x), jnp.float32), local, (0, BX * index)
    )
    interior = full.reshape(BZ + 1, BY + 1, vert_x)[1:BZ, 1:BY, 1 : vert_x - 1]
    for bit in range(int(math.log2(width))):
        partner = [(i, i ^ (1 << bit)) for i in range(width)]
        interior = interior + lax.ppermute(interior, "group", partner)
    return interior


def body(
    right_side,
    stiff_fine,
    smooth_fine,
    restrict_fine,
    stiff_middle,
    smooth_middle,
    restrict_middle,
    neighbor,
    send_group,
    send_region,
    ghost_orient,
    corners,
):
    tables = make_tables(neighbor, send_group, send_region, ghost_orient)
    width_group = lax.axis_size("group")
    index = lax.axis_index("group")
    vert_x = width_group * BX + 1
    planes = (BZ + 1) * (BY + 1)
    corner_ids = corners.T
    sent_ids = jnp.einsum(
        "nj,sjk->snk", corner_ids.astype(jnp.float32), tables[1], precision=HIGHEST,
        preferred_element_type=jnp.float32,
    )

    smoothed = mm(smooth_fine, right_side)
    operated, received = apply_level(smoothed, stiff_fine, FINE_PTS, tables, extra=sent_ids)
    residual = right_side - operated
    neighbor_ids = jnp.round(jnp.concatenate(received, axis=1)).astype(jnp.int32)
    middle_rhs = mm(restrict_fine, residual)
    middle_fix = mm(smooth_middle, middle_rhs)
    middle_res = middle_rhs - apply_level(middle_fix, stiff_middle, MID_PTS, tables)[0]
    corner_terms = mm(restrict_middle, middle_res)

    plane_ids = corner_ids.reshape(-1) // vert_x
    column = corner_ids.reshape(-1) - plane_ids * vert_x - BX * index
    on_plane = (plane_ids[None, :] == jnp.arange(planes, dtype=jnp.int32)[:, None]).astype(
        jnp.float32
    )
    on_column = (column[:, None] == jnp.arange(BX + 1, dtype=jnp.int32)[None, :]).astype(
        jnp.float32
    )
    local = mm(on_plane, corner_terms.reshape(-1)[:, None] * on_column)
    interior = gather_slab(local, width_group)
    solved = coarse_solve(interior)
    padded = jnp.pad(solved, ((1, 1), (1, 1), (1 + BX, 1 + BX)))
    window = lax.dynamic_slice_in_dim(padded, BX * index, 3 * BX + 1, axis=2)
    window = window.reshape(planes, 3 * BX + 1)
    mine = window[:, BX : 2 * BX + 1]
    coarse_fix = corner_values(mine, corner_ids, BX * index, planes, vert_x)
    neighbor_fix = corner_values(window, neighbor_ids, BX * (index - 1), planes, vert_x)
    face_select = trace_matrix(MID_PTS).reshape(6, MID_PTS**2, MID_PTS**3)
    neighbor_corr = mm(restrict_middle.T, neighbor_fix)
    count = send_group.shape[2]
    low_valid = (index > 0).astype(jnp.float32)
    high_valid = (index < width_group - 1).astype(jnp.float32)
    group_ghosts = (
        mm(jnp.asarray(face_select[1]), neighbor_corr[:, :count]) * low_valid,
        mm(jnp.asarray(face_select[0]), neighbor_corr[:, count:]) * high_valid,
    )

    correction = mm(restrict_middle.T, coarse_fix)
    middle_corr = middle_fix + correction
    middle_left = middle_res - apply_level(
        correction, stiff_middle, MID_PTS, tables, group_ghosts=group_ghosts
    )[0]
    middle_post = middle_corr + mm(smooth_middle, middle_left)
    current = smoothed + mm(restrict_fine.T, middle_post)
    left_over = right_side - apply_level(current, stiff_fine, FINE_PTS, tables)[0]
    return current + mm(smooth_fine, left_over)


def solution(mesh):
    return jax.shard_map(
        body,
        mesh=mesh,
        in_specs=(
            P(None, ("region", "group")),
            P(),
            P(),
            P(),
            P(),
            P(),
            P(),
            P(("region", "group"), None),
            P(("region", "group"), None, None),
            P(("region", "group"), None, None),
            P(("region", "group"), None),
            P(("region", "group"), None),
        ),
        out_specs=P(None, ("region", "group")),
        check_vma=False,
    )
```

```python
import math

import jax
import jax.numpy as jnp
import numpy as np
from jax import lax
from jax.sharding import PartitionSpec as P

FINE_PTS = 6
MID_PTS = 3
BX = 2
BY = 8
BZ = 24


HIGHEST = lax.Precision.HIGHEST
penalty_fine = 1.0
penalty_middle = 1.0


def mm(a, b):
    return jnp.dot(a, b, precision=HIGHEST, preferred_element_type=jnp.float32)


def orient_lookup(points):
    lookup = np.zeros((8, points * points), np.int32)
    for code_index in range(8):
        for row_index in range(points):
            for col_index in range(points):
                first_pos, second_pos = (row_index, col_index)
                if code_index >= 4:
                    first_pos, second_pos = (second_pos, first_pos)
                for rotation in range(code_index % 4):
                    first_pos, second_pos = (second_pos, points - 1 - first_pos)
                lookup[code_index, row_index * points + col_index] = first_pos * points + second_pos
    return lookup


def orient_matrix(points):
    lookup = orient_lookup(points)
    plane = points * points
    mat = np.zeros((8 * plane, plane), np.float32)
    for code_index in range(8):
        mat[code_index * plane + np.arange(plane), lookup[code_index]] = 1.0
    return mat


def face_nodes(points):
    ids = np.arange(points**3).reshape(points, points, points)
    last = points - 1
    pieces = [ids[0], ids[last], ids[:, 0], ids[:, last], ids[:, :, 0], ids[:, :, last]]
    return np.stack([p.reshape(-1) for p in pieces])


def trace_matrix(points):
    nodes = face_nodes(points)
    plane = points * points
    mat = np.zeros((6 * plane, points**3), np.float32)
    for face_index in range(6):
        mat[face_index * plane + np.arange(plane), nodes[face_index]] = 1.0
    return mat


def make_tables(neighbor, send_group, send_region, ghost_orient):
    elements = neighbor.shape[0]
    group_count = send_group.shape[2]
    region_count = send_region.shape[2]
    ghosts = 2 * group_count + 2 * region_count
    slots = jnp.arange(elements, dtype=jnp.int32)
    sources = jnp.arange(elements + ghosts, dtype=jnp.int32)
    gather = (neighbor.T[:, None, :] == sources[None, :, None]).astype(jnp.bfloat16)
    pick_group = (send_group[0][:, None, :] == slots[None, :, None]).astype(jnp.float32)
    pick_region = (send_region[0][:, None, :] == slots[None, :, None]).astype(jnp.float32)
    codes = (ghost_orient[0][None, :] == jnp.arange(8, dtype=jnp.int32)[:, None]).astype(
        jnp.float32
    )
    return gather, pick_group, pick_region, codes


def shift(block, axis, step):
    count = lax.axis_size(axis)
    if step > 0:
        pairs = [(i, i + 1) for i in range(count - 1)]
    else:
        pairs = [(i + 1, i) for i in range(count - 1)]
    return lax.ppermute(block, axis, pairs)


def region_exchange(region_out):
    count = lax.axis_size("region")
    odd = (lax.axis_index("region") % 2) == 1
    far_pairs = [(i, i + 1) for i in range(1, count - 1, 2)]
    far_pairs += [(i, i - 1) for i in range(2, count, 2)]
    near_pairs = [(i, i + 1) for i in range(0, count - 1, 2)]
    near_pairs += [(i + 1, i) for i in range(0, count - 1, 2)]
    far_recv = lax.ppermute(
        jnp.where(odd, region_out[1], region_out[0]), "region", far_pairs
    )
    near_recv = lax.ppermute(
        jnp.where(odd, region_out[0], region_out[1]), "region", near_pairs
    )
    return jnp.where(odd, near_recv, far_recv), jnp.where(odd, far_recv, near_recv)


def apply_level(current, stiffness, points, tables, extra=None, group_ghosts=None):
    gather, pick_group, pick_region, codes = tables
    plane = points * points
    cube = points**3
    elements = current.shape[1]
    select = jnp.asarray(trace_matrix(points))
    both = mm(jnp.concatenate([stiffness, select], axis=0), current)
    product = both[:cube]
    traces = both[cube:].reshape(6, plane, elements)
    region_out = jnp.einsum(
        "snj,sjk->snk", traces[2:4], pick_region, precision=HIGHEST,
        preferred_element_type=jnp.float32,
    )
    from_region_low, from_region_high = region_exchange(region_out)
    received = None
    if group_ghosts is None:
        group_out = jnp.einsum(
            "snj,sjk->snk", traces[0:2], pick_group, precision=HIGHEST,
            preferred_element_type=jnp.float32,
        )
        if extra is not None:
            group_out = jnp.concatenate([group_out, extra], axis=1)
        from_group_low = shift(group_out[1], "group", 1)
        from_group_high = shift(group_out[0], "group", -1)
        received = (from_group_low[plane:], from_group_high[plane:])
        group_ghosts = (from_group_low[:plane], from_group_high[:plane])
    raw = jnp.concatenate(
        [group_ghosts[0], group_ghosts[1], from_region_low, from_region_high], axis=1
    )
    turned = mm(jnp.asarray(orient_matrix(points)), raw).reshape(8, plane, -1)
    ghosts = jnp.sum(turned * codes[:, None, :], axis=0)
    swapped = traces[np.array([1, 0, 3, 2, 5, 4])]
    source = jnp.concatenate(
        [swapped, jnp.broadcast_to(ghosts[None], (6,) + ghosts.shape)], axis=2
    )
    outside = jnp.einsum(
        "fnq,fqe->fne", source, gather.astype(jnp.float32), precision=HIGHEST,
        preferred_element_type=jnp.float32,
    )
    jumps = (traces - outside).reshape(6 * plane, elements)
    return product + mm(select.T, jumps), received


def corner_values(window, ids, first_column, planes, vert_x):
    flat = ids.reshape(-1)
    plane_ids = flat // vert_x
    column = flat - plane_ids * vert_x - first_column
    on_plane = (plane_ids[None, :] == jnp.arange(planes, dtype=jnp.int32)[:, None]).astype(
        jnp.float32
    )
    on_column = (
        column[:, None] == jnp.arange(window.shape[1], dtype=jnp.int32)[None, :]
    ).astype(jnp.float32)
    picked = mm(window.T, on_plane)
    return jnp.sum(picked * on_column.T, axis=0).reshape(ids.shape)


def sine_basis(extent):
    ordinal = jnp.arange(1, extent + 1, dtype=jnp.int32)
    wrapped = ordinal[:, None] * ordinal[None, :] % (2 * (extent + 1))
    return math.sqrt(2.0 / (extent + 1)) * jnp.sin(
        wrapped.astype(jnp.float32) * (math.pi / (extent + 1))
    )


def spectrum(extent):
    cosine = jnp.cos(
        jnp.arange(1, extent + 1, dtype=jnp.int32).astype(jnp.float32) * (math.pi / (extent + 1))
    )
    return (2.0 - 2.0 * cosine, (4.0 + 2.0 * cosine) / 6.0)


def transform(volume, basis_z, basis_y, basis_x):
    turned = jnp.einsum("zyx,xk->zyk", volume, basis_x, precision=HIGHEST)
    turned = jnp.einsum("zyk,yj->zjk", turned, basis_y, precision=HIGHEST)
    return jnp.einsum("zjk,zi->ijk", turned, basis_z, precision=HIGHEST)


def coarse_solve(interior):
    depth_count, height_count, breadth_count = interior.shape
    basis_z, basis_y, basis_x = (
        sine_basis(depth_count),
        sine_basis(height_count),
        sine_basis(breadth_count),
    )
    stiff_z, mass_z = spectrum(depth_count)
    stiff_y, mass_y = spectrum(height_count)
    stiff_x, mass_x = spectrum(breadth_count)
    eigen_sum = (
        stiff_z[:, None, None] * mass_y[None, :, None] * mass_x[None, None, :]
        + mass_z[:, None, None] * stiff_y[None, :, None] * mass_x[None, None, :]
        + mass_z[:, None, None] * mass_y[None, :, None] * stiff_x[None, None, :]
    )
    return transform(
        transform(interior, basis_z, basis_y, basis_x) / eigen_sum, basis_z, basis_y, basis_x
    )


def gather_slab(local, width):
    index = lax.axis_index("group")
    vert_x = BX * width + 1
    full = lax.dynamic_update_slice(
        jnp.zeros((local.shape[0], vert_x), jnp.float32), local, (0, BX * index)
    )
    interior = full.reshape(BZ + 1, BY + 1, vert_x)[1:BZ, 1:BY, 1 : vert_x - 1]
    for bit in range(int(math.log2(width))):
        partner = [(i, i ^ (1 << bit)) for i in range(width)]
        interior = interior + lax.ppermute(interior, "group", partner)
    return interior


def body(
    right_side,
    stiff_fine,
    smooth_fine,
    restrict_fine,
    stiff_middle,
    smooth_middle,
    restrict_middle,
    neighbor,
    send_group,
    send_region,
    ghost_orient,
    corners,
):
    tables = make_tables(neighbor, send_group, send_region, ghost_orient)
    width_group = lax.axis_size("group")
    index = lax.axis_index("group")
    vert_x = width_group * BX + 1
    planes = (BZ + 1) * (BY + 1)
    corner_ids = corners.T
    sent_ids = jnp.einsum(
        "nj,sjk->snk", corner_ids.astype(jnp.float32), tables[1], precision=HIGHEST,
        preferred_element_type=jnp.float32,
    )

    smoothed = mm(smooth_fine, right_side)
    operated, received = apply_level(smoothed, stiff_fine, FINE_PTS, tables, extra=sent_ids)
    residual = right_side - operated
    neighbor_ids = jnp.round(jnp.concatenate(received, axis=1)).astype(jnp.int32)
    middle_rhs = mm(restrict_fine, residual)
    middle_fix = mm(smooth_middle, middle_rhs)
    middle_res = middle_rhs - apply_level(middle_fix, stiff_middle, MID_PTS, tables)[0]
    corner_terms = mm(restrict_middle, middle_res)

    plane_ids = corner_ids.reshape(-1) // vert_x
    column = corner_ids.reshape(-1) - plane_ids * vert_x - BX * index
    on_plane = (plane_ids[None, :] == jnp.arange(planes, dtype=jnp.int32)[:, None]).astype(
        jnp.float32
    )
    on_column = (column[:, None] == jnp.arange(BX + 1, dtype=jnp.int32)[None, :]).astype(
        jnp.float32
    )
    local = mm(on_plane, corner_terms.reshape(-1)[:, None] * on_column)
    interior = gather_slab(local, width_group)
    solved = coarse_solve(interior)
    padded = jnp.pad(solved, ((1, 1), (1, 1), (1 + BX, 1 + BX)))
    window = lax.dynamic_slice_in_dim(padded, BX * index, 3 * BX + 1, axis=2)
    window = window.reshape(planes, 3 * BX + 1)
    mine = window[:, BX : 2 * BX + 1]
    coarse_fix = corner_values(mine, corner_ids, BX * index, planes, vert_x)
    neighbor_fix = corner_values(window, neighbor_ids, BX * (index - 1), planes, vert_x)
    face_select = trace_matrix(MID_PTS).reshape(6, MID_PTS**2, MID_PTS**3)
    neighbor_corr = mm(restrict_middle.T, neighbor_fix)
    count = send_group.shape[2]
    low_valid = (index > 0).astype(jnp.float32)
    high_valid = (index < width_group - 1).astype(jnp.float32)
    group_ghosts = (
        mm(jnp.asarray(face_select[1]), neighbor_corr[:, :count]) * low_valid,
        mm(jnp.asarray(face_select[0]), neighbor_corr[:, count:]) * high_valid,
    )

    correction = mm(restrict_middle.T, coarse_fix)
    middle_corr = middle_fix + correction
    middle_left = middle_res - apply_level(
        correction, stiff_middle, MID_PTS, tables, group_ghosts=group_ghosts
    )[0]
    middle_post = middle_corr + mm(smooth_middle, middle_left)
    current = smoothed + mm(restrict_fine.T, middle_post)
    left_over = right_side - apply_level(current, stiff_fine, FINE_PTS, tables)[0]
    return current + mm(smooth_fine, left_over)


def solution(mesh):
    return jax.shard_map(
        body,
        mesh=mesh,
        in_specs=(
            P(None, ("region", "group")),
            P(),
            P(),
            P(),
            P(),
            P(),
            P(),
            P(("region", "group"), None),
            P(("region", "group"), None, None),
            P(("region", "group"), None, None),
            P(("region", "group"), None),
            P(("region", "group"), None),
        ),
        out_specs=P(None, ("region", "group")),
        check_vma=False,
    )
```

```python
import math

import jax
import jax.numpy as jnp
import numpy as np
from jax import lax
from jax.sharding import PartitionSpec as P

FINE_PTS = 6
MID_PTS = 3
BX = 2
BY = 8
BZ = 24


HIGHEST = lax.Precision.HIGHEST
HIGH = lax.Precision.HIGH
penalty_fine = 1.0
penalty_middle = 1.0


def mm(a, b):
    return jnp.dot(a, b, precision=HIGHEST, preferred_element_type=jnp.float32)


def pick(a, b):
    return jnp.dot(a, b, precision=HIGH, preferred_element_type=jnp.float32)


def orient_lookup(points):
    lookup = np.zeros((8, points * points), np.int32)
    for code_index in range(8):
        for row_index in range(points):
            for col_index in range(points):
                first_pos, second_pos = (row_index, col_index)
                if code_index >= 4:
                    first_pos, second_pos = (second_pos, first_pos)
                for rotation in range(code_index % 4):
                    first_pos, second_pos = (second_pos, points - 1 - first_pos)
                lookup[code_index, row_index * points + col_index] = first_pos * points + second_pos
    return lookup


def orient_matrix(points):
    lookup = orient_lookup(points)
    plane = points * points
    mat = np.zeros((8 * plane, plane), np.float32)
    for code_index in range(8):
        mat[code_index * plane + np.arange(plane), lookup[code_index]] = 1.0
    return mat


def face_nodes(points):
    ids = np.arange(points**3).reshape(points, points, points)
    last = points - 1
    pieces = [ids[0], ids[last], ids[:, 0], ids[:, last], ids[:, :, 0], ids[:, :, last]]
    return np.stack([p.reshape(-1) for p in pieces])


def trace_matrix(points):
    nodes = face_nodes(points)
    plane = points * points
    mat = np.zeros((6 * plane, points**3), np.float32)
    for face_index in range(6):
        mat[face_index * plane + np.arange(plane), nodes[face_index]] = 1.0
    return mat


def make_tables(neighbor, send_group, send_region, ghost_orient):
    elements = neighbor.shape[0]
    group_count = send_group.shape[2]
    region_count = send_region.shape[2]
    ghosts = 2 * group_count + 2 * region_count
    slots = jnp.arange(elements, dtype=jnp.int32)
    sources = jnp.arange(elements + ghosts, dtype=jnp.int32)
    gather = (neighbor.T[:, None, :] == sources[None, :, None]).astype(jnp.bfloat16)
    pick_group = (send_group[0][:, None, :] == slots[None, :, None]).astype(jnp.float32)
    pick_region = (send_region[0][:, None, :] == slots[None, :, None]).astype(jnp.float32)
    codes = (ghost_orient[0][None, :] == jnp.arange(8, dtype=jnp.int32)[:, None]).astype(
        jnp.float32
    )
    return gather, pick_group, pick_region, codes


def shift(block, axis, step):
    count = lax.axis_size(axis)
    if step > 0:
        pairs = [(i, i + 1) for i in range(count - 1)]
    else:
        pairs = [(i + 1, i) for i in range(count - 1)]
    return lax.ppermute(block, axis, pairs)


def region_exchange(region_out):
    count = lax.axis_size("region")
    odd = (lax.axis_index("region") % 2) == 1
    far_pairs = [(i, i + 1) for i in range(1, count - 1, 2)]
    far_pairs += [(i, i - 1) for i in range(2, count, 2)]
    near_pairs = [(i, i + 1) for i in range(0, count - 1, 2)]
    near_pairs += [(i + 1, i) for i in range(0, count - 1, 2)]
    far_recv = lax.ppermute(
        jnp.where(odd, region_out[1], region_out[0]), "region", far_pairs
    )
    near_recv = lax.ppermute(
        jnp.where(odd, region_out[0], region_out[1]), "region", near_pairs
    )
    return jnp.where(odd, near_recv, far_recv), jnp.where(odd, far_recv, near_recv)


def apply_level(current, stiffness, points, tables, extra=None, group_ghosts=None):
    gather, pick_group, pick_region, codes = tables
    plane = points * points
    cube = points**3
    elements = current.shape[1]
    select = jnp.asarray(trace_matrix(points))
    both = mm(jnp.concatenate([stiffness, select], axis=0), current)
    product = both[:cube]
    traces = both[cube:].reshape(6, plane, elements)
    region_out = jnp.einsum(
        "snj,sjk->snk", traces[2:4], pick_region, precision=HIGH,
        preferred_element_type=jnp.float32,
    )
    from_region_low, from_region_high = region_exchange(region_out)
    received = None
    if group_ghosts is None:
        group_out = jnp.einsum(
            "snj,sjk->snk", traces[0:2], pick_group, precision=HIGH,
            preferred_element_type=jnp.float32,
        )
        if extra is not None:
            group_out = jnp.concatenate([group_out, extra], axis=1)
        from_group_low = shift(group_out[1], "group", 1)
        from_group_high = shift(group_out[0], "group", -1)
        received = (from_group_low[plane:], from_group_high[plane:])
        group_ghosts = (from_group_low[:plane], from_group_high[:plane])
    raw = jnp.concatenate(
        [group_ghosts[0], group_ghosts[1], from_region_low, from_region_high], axis=1
    )
    turned = pick(jnp.asarray(orient_matrix(points)), raw).reshape(8, plane, -1)
    ghosts = jnp.sum(turned * codes[:, None, :], axis=0)
    swapped = traces[np.array([1, 0, 3, 2, 5, 4])]
    source = jnp.concatenate(
        [swapped, jnp.broadcast_to(ghosts[None], (6,) + ghosts.shape)], axis=2
    )
    outside = jnp.einsum(
        "fnq,fqe->fne", source, gather.astype(jnp.float32), precision=HIGH,
        preferred_element_type=jnp.float32,
    )
    jumps = (traces - outside).reshape(6 * plane, elements)
    return product + pick(select.T, jumps), received


def corner_values(window, ids, first_column, planes, vert_x):
    flat = ids.reshape(-1)
    plane_ids = flat // vert_x
    column = flat - plane_ids * vert_x - first_column
    on_plane = (plane_ids[None, :] == jnp.arange(planes, dtype=jnp.int32)[:, None]).astype(
        jnp.float32
    )
    on_column = (
        column[:, None] == jnp.arange(window.shape[1], dtype=jnp.int32)[None, :]
    ).astype(jnp.float32)
    picked = pick(window.T, on_plane)
    return jnp.sum(picked * on_column.T, axis=0).reshape(ids.shape)


def sine_basis(extent):
    ordinal = jnp.arange(1, extent + 1, dtype=jnp.int32)
    wrapped = ordinal[:, None] * ordinal[None, :] % (2 * (extent + 1))
    return math.sqrt(2.0 / (extent + 1)) * jnp.sin(
        wrapped.astype(jnp.float32) * (math.pi / (extent + 1))
    )


def spectrum(extent):
    cosine = jnp.cos(
        jnp.arange(1, extent + 1, dtype=jnp.int32).astype(jnp.float32) * (math.pi / (extent + 1))
    )
    return (2.0 - 2.0 * cosine, (4.0 + 2.0 * cosine) / 6.0)


def transform(volume, basis_z, basis_y, basis_x):
    turned = jnp.einsum("zyx,xk->zyk", volume, basis_x, precision=HIGHEST)
    turned = jnp.einsum("zyk,yj->zjk", turned, basis_y, precision=HIGHEST)
    return jnp.einsum("zjk,zi->ijk", turned, basis_z, precision=HIGHEST)


def coarse_solve(interior):
    depth_count, height_count, breadth_count = interior.shape
    basis_z, basis_y, basis_x = (
        sine_basis(depth_count),
        sine_basis(height_count),
        sine_basis(breadth_count),
    )
    stiff_z, mass_z = spectrum(depth_count)
    stiff_y, mass_y = spectrum(height_count)
    stiff_x, mass_x = spectrum(breadth_count)
    eigen_sum = (
        stiff_z[:, None, None] * mass_y[None, :, None] * mass_x[None, None, :]
        + mass_z[:, None, None] * stiff_y[None, :, None] * mass_x[None, None, :]
        + mass_z[:, None, None] * mass_y[None, :, None] * stiff_x[None, None, :]
    )
    return transform(
        transform(interior, basis_z, basis_y, basis_x) / eigen_sum, basis_z, basis_y, basis_x
    )


def gather_slab(local, width):
    index = lax.axis_index("group")
    vert_x = BX * width + 1
    full = lax.dynamic_update_slice(
        jnp.zeros((local.shape[0], vert_x), jnp.float32), local, (0, BX * index)
    )
    interior = full.reshape(BZ + 1, BY + 1, vert_x)[1:BZ, 1:BY, 1 : vert_x - 1]
    for bit in range(int(math.log2(width))):
        partner = [(i, i ^ (1 << bit)) for i in range(width)]
        interior = interior + lax.ppermute(interior, "group", partner)
    return interior


def body(
    right_side,
    stiff_fine,
    smooth_fine,
    restrict_fine,
    stiff_middle,
    smooth_middle,
    restrict_middle,
    neighbor,
    send_group,
    send_region,
    ghost_orient,
    corners,
):
    tables = make_tables(neighbor, send_group, send_region, ghost_orient)
    width_group = lax.axis_size("group")
    index = lax.axis_index("group")
    vert_x = width_group * BX + 1
    planes = (BZ + 1) * (BY + 1)
    corner_ids = corners.T
    sent_ids = jnp.einsum(
        "nj,sjk->snk", corner_ids.astype(jnp.float32), tables[1], precision=HIGHEST,
        preferred_element_type=jnp.float32,
    )

    smoothed = mm(smooth_fine, right_side)
    operated, received = apply_level(smoothed, stiff_fine, FINE_PTS, tables, extra=sent_ids)
    residual = right_side - operated
    neighbor_ids = jnp.round(jnp.concatenate(received, axis=1)).astype(jnp.int32)
    middle_rhs = mm(restrict_fine, residual)
    middle_fix = mm(smooth_middle, middle_rhs)
    middle_res = middle_rhs - apply_level(middle_fix, stiff_middle, MID_PTS, tables)[0]
    corner_terms = mm(restrict_middle, middle_res)

    plane_ids = corner_ids.reshape(-1) // vert_x
    column = corner_ids.reshape(-1) - plane_ids * vert_x - BX * index
    on_plane = (plane_ids[None, :] == jnp.arange(planes, dtype=jnp.int32)[:, None]).astype(
        jnp.float32
    )
    on_column = (column[:, None] == jnp.arange(BX + 1, dtype=jnp.int32)[None, :]).astype(
        jnp.float32
    )
    local = pick(on_plane, corner_terms.reshape(-1)[:, None] * on_column)
    interior = gather_slab(local, width_group)
    solved = coarse_solve(interior)
    padded = jnp.pad(solved, ((1, 1), (1, 1), (1 + BX, 1 + BX)))
    window = lax.dynamic_slice_in_dim(padded, BX * index, 3 * BX + 1, axis=2)
    window = window.reshape(planes, 3 * BX + 1)
    mine = window[:, BX : 2 * BX + 1]
    coarse_fix = corner_values(mine, corner_ids, BX * index, planes, vert_x)
    neighbor_fix = corner_values(window, neighbor_ids, BX * (index - 1), planes, vert_x)
    face_select = trace_matrix(MID_PTS).reshape(6, MID_PTS**2, MID_PTS**3)
    neighbor_corr = mm(restrict_middle.T, neighbor_fix)
    count = send_group.shape[2]
    low_valid = (index > 0).astype(jnp.float32)
    high_valid = (index < width_group - 1).astype(jnp.float32)
    group_ghosts = (
        mm(jnp.asarray(face_select[1]), neighbor_corr[:, :count]) * low_valid,
        mm(jnp.asarray(face_select[0]), neighbor_corr[:, count:]) * high_valid,
    )

    correction = mm(restrict_middle.T, coarse_fix)
    middle_corr = middle_fix + correction
    middle_left = middle_res - apply_level(
        correction, stiff_middle, MID_PTS, tables, group_ghosts=group_ghosts
    )[0]
    middle_post = middle_corr + mm(smooth_middle, middle_left)
    current = smoothed + mm(restrict_fine.T, middle_post)
    left_over = right_side - apply_level(current, stiff_fine, FINE_PTS, tables)[0]
    return current + mm(smooth_fine, left_over)


def solution(mesh):
    return jax.shard_map(
        body,
        mesh=mesh,
        in_specs=(
            P(None, ("region", "group")),
            P(),
            P(),
            P(),
            P(),
            P(),
            P(),
            P(("region", "group"), None),
            P(("region", "group"), None, None),
            P(("region", "group"), None, None),
            P(("region", "group"), None),
            P(("region", "group"), None),
        ),
        out_specs=P(None, ("region", "group")),
        check_vma=False,
    )
```

```python
import math

import jax
import jax.numpy as jnp
import numpy as np
from jax import lax
from jax.sharding import PartitionSpec as P

FINE_PTS = 6
MID_PTS = 3
BX = 2
BY = 8
BZ = 24


HIGHEST = lax.Precision.HIGHEST
HIGH = lax.Precision.HIGH
penalty_fine = 1.0
penalty_middle = 1.0


def mm(a, b):
    return jnp.dot(a, b, precision=HIGHEST, preferred_element_type=jnp.float32)


def pick(a, b):
    return jnp.dot(a, b, precision=HIGH, preferred_element_type=jnp.float32)


def orient_lookup(points):
    lookup = np.zeros((8, points * points), np.int32)
    for code_index in range(8):
        for row_index in range(points):
            for col_index in range(points):
                first_pos, second_pos = (row_index, col_index)
                if code_index >= 4:
                    first_pos, second_pos = (second_pos, first_pos)
                for rotation in range(code_index % 4):
                    first_pos, second_pos = (second_pos, points - 1 - first_pos)
                lookup[code_index, row_index * points + col_index] = first_pos * points + second_pos
    return lookup


def orient_matrix(points):
    lookup = orient_lookup(points)
    plane = points * points
    mat = np.zeros((8 * plane, plane), np.float32)
    for code_index in range(8):
        mat[code_index * plane + np.arange(plane), lookup[code_index]] = 1.0
    return mat


def face_nodes(points):
    ids = np.arange(points**3).reshape(points, points, points)
    last = points - 1
    pieces = [ids[0], ids[last], ids[:, 0], ids[:, last], ids[:, :, 0], ids[:, :, last]]
    return np.stack([p.reshape(-1) for p in pieces])


def trace_matrix(points):
    nodes = face_nodes(points)
    plane = points * points
    mat = np.zeros((6 * plane, points**3), np.float32)
    for face_index in range(6):
        mat[face_index * plane + np.arange(plane), nodes[face_index]] = 1.0
    return mat


def make_tables(neighbor, send_group, send_region, ghost_orient):
    elements = neighbor.shape[0]
    group_count = send_group.shape[2]
    region_count = send_region.shape[2]
    ghosts = 2 * group_count + 2 * region_count
    slots = jnp.arange(elements, dtype=jnp.int32)
    sources = jnp.arange(elements + ghosts, dtype=jnp.int32)
    gather = (neighbor.T[:, None, :] == sources[None, :, None]).astype(jnp.bfloat16)
    pick_group = (send_group[0][:, None, :] == slots[None, :, None]).astype(jnp.float32)
    pick_region = (send_region[0][:, None, :] == slots[None, :, None]).astype(jnp.float32)
    codes = (ghost_orient[0][None, :] == jnp.arange(8, dtype=jnp.int32)[:, None]).astype(
        jnp.float32
    )
    return gather, pick_group, pick_region, codes


def shift(block, axis, step):
    count = lax.axis_size(axis)
    if step > 0:
        pairs = [(i, i + 1) for i in range(count - 1)]
    else:
        pairs = [(i + 1, i) for i in range(count - 1)]
    return lax.ppermute(block, axis, pairs)


def region_exchange(region_out):
    count = lax.axis_size("region")
    odd = (lax.axis_index("region") % 2) == 1
    far_pairs = [(i, i + 1) for i in range(1, count - 1, 2)]
    far_pairs += [(i, i - 1) for i in range(2, count, 2)]
    near_pairs = [(i, i + 1) for i in range(0, count - 1, 2)]
    near_pairs += [(i + 1, i) for i in range(0, count - 1, 2)]
    near_recv = lax.ppermute(
        jnp.where(odd, region_out[0], region_out[1]), "region", near_pairs
    )
    far_recv = lax.ppermute(
        jnp.where(odd, region_out[1], region_out[0]), "region", far_pairs
    )
    return jnp.where(odd, near_recv, far_recv), jnp.where(odd, far_recv, near_recv)


def apply_level(current, stiffness, points, tables, extra=None, group_ghosts=None):
    gather, pick_group, pick_region, codes = tables
    plane = points * points
    cube = points**3
    elements = current.shape[1]
    select = jnp.asarray(trace_matrix(points))
    both = mm(jnp.concatenate([stiffness, select], axis=0), current)
    product = both[:cube]
    traces = both[cube:].reshape(6, plane, elements)
    region_out = jnp.einsum(
        "snj,sjk->snk", traces[2:4], pick_region, precision=HIGH,
        preferred_element_type=jnp.float32,
    )
    from_region_low, from_region_high = region_exchange(region_out)
    received = None
    if group_ghosts is None:
        group_out = jnp.einsum(
            "snj,sjk->snk", traces[0:2], pick_group, precision=HIGH,
            preferred_element_type=jnp.float32,
        )
        if extra is not None:
            group_out = jnp.concatenate([group_out, extra], axis=1)
        from_group_low = shift(group_out[1], "group", 1)
        from_group_high = shift(group_out[0], "group", -1)
        received = (from_group_low[plane:], from_group_high[plane:])
        group_ghosts = (from_group_low[:plane], from_group_high[:plane])
    raw = jnp.concatenate(
        [group_ghosts[0], group_ghosts[1], from_region_low, from_region_high], axis=1
    )
    turned = pick(jnp.asarray(orient_matrix(points)), raw).reshape(8, plane, -1)
    ghosts = jnp.sum(turned * codes[:, None, :], axis=0)
    swapped = traces[np.array([1, 0, 3, 2, 5, 4])]
    source = jnp.concatenate(
        [swapped, jnp.broadcast_to(ghosts[None], (6,) + ghosts.shape)], axis=2
    )
    outside = jnp.einsum(
        "fnq,fqe->fne", source, gather.astype(jnp.float32), precision=HIGH,
        preferred_element_type=jnp.float32,
    )
    jumps = (traces - outside).reshape(6 * plane, elements)
    return product + pick(select.T, jumps), received


def corner_values(window, ids, first_column, planes, vert_x):
    flat = ids.reshape(-1)
    plane_ids = flat // vert_x
    column = flat - plane_ids * vert_x - first_column
    on_plane = (plane_ids[None, :] == jnp.arange(planes, dtype=jnp.int32)[:, None]).astype(
        jnp.float32
    )
    on_column = (
        column[:, None] == jnp.arange(window.shape[1], dtype=jnp.int32)[None, :]
    ).astype(jnp.float32)
    picked = pick(window.T, on_plane)
    return jnp.sum(picked * on_column.T, axis=0).reshape(ids.shape)


def sine_basis(extent):
    ordinal = jnp.arange(1, extent + 1, dtype=jnp.int32)
    wrapped = ordinal[:, None] * ordinal[None, :] % (2 * (extent + 1))
    return math.sqrt(2.0 / (extent + 1)) * jnp.sin(
        wrapped.astype(jnp.float32) * (math.pi / (extent + 1))
    )


def spectrum(extent):
    cosine = jnp.cos(
        jnp.arange(1, extent + 1, dtype=jnp.int32).astype(jnp.float32) * (math.pi / (extent + 1))
    )
    return (2.0 - 2.0 * cosine, (4.0 + 2.0 * cosine) / 6.0)


def transform(volume, basis_z, basis_y, basis_x):
    turned = jnp.einsum("zyx,xk->zyk", volume, basis_x, precision=HIGHEST)
    turned = jnp.einsum("zyk,yj->zjk", turned, basis_y, precision=HIGHEST)
    return jnp.einsum("zjk,zi->ijk", turned, basis_z, precision=HIGHEST)


def coarse_solve(interior):
    depth_count, height_count, breadth_count = interior.shape
    basis_z, basis_y, basis_x = (
        sine_basis(depth_count),
        sine_basis(height_count),
        sine_basis(breadth_count),
    )
    stiff_z, mass_z = spectrum(depth_count)
    stiff_y, mass_y = spectrum(height_count)
    stiff_x, mass_x = spectrum(breadth_count)
    eigen_sum = (
        stiff_z[:, None, None] * mass_y[None, :, None] * mass_x[None, None, :]
        + mass_z[:, None, None] * stiff_y[None, :, None] * mass_x[None, None, :]
        + mass_z[:, None, None] * mass_y[None, :, None] * stiff_x[None, None, :]
    )
    return transform(
        transform(interior, basis_z, basis_y, basis_x) / eigen_sum, basis_z, basis_y, basis_x
    )


def gather_slab(local, width):
    index = lax.axis_index("group")
    vert_x = BX * width + 1
    full = lax.dynamic_update_slice(
        jnp.zeros((local.shape[0], vert_x), jnp.float32), local, (0, BX * index)
    )
    interior = full.reshape(BZ + 1, BY + 1, vert_x)[1:BZ, 1:BY, 1 : vert_x - 1]
    for bit in range(int(math.log2(width))):
        partner = [(i, i ^ (1 << bit)) for i in range(width)]
        interior = interior + lax.ppermute(interior, "group", partner)
    return interior


def body(
    right_side,
    stiff_fine,
    smooth_fine,
    restrict_fine,
    stiff_middle,
    smooth_middle,
    restrict_middle,
    neighbor,
    send_group,
    send_region,
    ghost_orient,
    corners,
):
    tables = make_tables(neighbor, send_group, send_region, ghost_orient)
    width_group = lax.axis_size("group")
    index = lax.axis_index("group")
    vert_x = width_group * BX + 1
    planes = (BZ + 1) * (BY + 1)
    corner_ids = corners.T
    sent_ids = jnp.einsum(
        "nj,sjk->snk", corner_ids.astype(jnp.float32), tables[1], precision=HIGHEST,
        preferred_element_type=jnp.float32,
    )

    smoothed = mm(smooth_fine, right_side)
    operated, received = apply_level(smoothed, stiff_fine, FINE_PTS, tables, extra=sent_ids)
    residual = right_side - operated
    neighbor_ids = jnp.round(jnp.concatenate(received, axis=1)).astype(jnp.int32)
    middle_rhs = mm(restrict_fine, residual)
    middle_fix = mm(smooth_middle, middle_rhs)
    middle_res = middle_rhs - apply_level(middle_fix, stiff_middle, MID_PTS, tables)[0]
    corner_terms = mm(restrict_middle, middle_res)

    plane_ids = corner_ids.reshape(-1) // vert_x
    column = corner_ids.reshape(-1) - plane_ids * vert_x - BX * index
    on_plane = (plane_ids[None, :] == jnp.arange(planes, dtype=jnp.int32)[:, None]).astype(
        jnp.float32
    )
    on_column = (column[:, None] == jnp.arange(BX + 1, dtype=jnp.int32)[None, :]).astype(
        jnp.float32
    )
    local = pick(on_plane, corner_terms.reshape(-1)[:, None] * on_column)
    interior = gather_slab(local, width_group)
    solved = coarse_solve(interior)
    padded = jnp.pad(solved, ((1, 1), (1, 1), (1 + BX, 1 + BX)))
    window = lax.dynamic_slice_in_dim(padded, BX * index, 3 * BX + 1, axis=2)
    window = window.reshape(planes, 3 * BX + 1)
    mine = window[:, BX : 2 * BX + 1]
    coarse_fix = corner_values(mine, corner_ids, BX * index, planes, vert_x)
    neighbor_fix = corner_values(window, neighbor_ids, BX * (index - 1), planes, vert_x)
    face_select = trace_matrix(MID_PTS).reshape(6, MID_PTS**2, MID_PTS**3)
    neighbor_corr = mm(restrict_middle.T, neighbor_fix)
    count = send_group.shape[2]
    low_valid = (index > 0).astype(jnp.float32)
    high_valid = (index < width_group - 1).astype(jnp.float32)
    group_ghosts = (
        mm(jnp.asarray(face_select[1]), neighbor_corr[:, :count]) * low_valid,
        mm(jnp.asarray(face_select[0]), neighbor_corr[:, count:]) * high_valid,
    )

    correction = mm(restrict_middle.T, coarse_fix)
    middle_corr = middle_fix + correction
    middle_left = middle_res - apply_level(
        correction, stiff_middle, MID_PTS, tables, group_ghosts=group_ghosts
    )[0]
    middle_post = middle_corr + mm(smooth_middle, middle_left)
    current = smoothed + mm(restrict_fine.T, middle_post)
    left_over = right_side - apply_level(current, stiff_fine, FINE_PTS, tables)[0]
    return current + mm(smooth_fine, left_over)


def solution(mesh):
    return jax.shard_map(
        body,
        mesh=mesh,
        in_specs=(
            P(None, ("region", "group")),
            P(),
            P(),
            P(),
            P(),
            P(),
            P(),
            P(("region", "group"), None),
            P(("region", "group"), None, None),
            P(("region", "group"), None, None),
            P(("region", "group"), None),
            P(("region", "group"), None),
        ),
        out_specs=P(None, ("region", "group")),
        check_vma=False,
    )
```

```python
import math

import jax
import jax.numpy as jnp
import numpy as np
from jax import lax
from jax.sharding import PartitionSpec as P

FINE_PTS = 6
MID_PTS = 3
BX = 2
BY = 8
BZ = 24


HIGHEST = lax.Precision.HIGHEST
HIGH = lax.Precision.HIGH
penalty_fine = 1.0
penalty_middle = 1.0


def mm(a, b):
    return jnp.dot(a, b, precision=HIGH, preferred_element_type=jnp.float32)


def pick(a, b):
    return jnp.dot(a, b, precision=HIGH, preferred_element_type=jnp.float32)


def orient_lookup(points):
    lookup = np.zeros((8, points * points), np.int32)
    for code_index in range(8):
        for row_index in range(points):
            for col_index in range(points):
                first_pos, second_pos = (row_index, col_index)
                if code_index >= 4:
                    first_pos, second_pos = (second_pos, first_pos)
                for rotation in range(code_index % 4):
                    first_pos, second_pos = (second_pos, points - 1 - first_pos)
                lookup[code_index, row_index * points + col_index] = first_pos * points + second_pos
    return lookup


def orient_matrix(points):
    lookup = orient_lookup(points)
    plane = points * points
    mat = np.zeros((8 * plane, plane), np.float32)
    for code_index in range(8):
        mat[code_index * plane + np.arange(plane), lookup[code_index]] = 1.0
    return mat


def face_nodes(points):
    ids = np.arange(points**3).reshape(points, points, points)
    last = points - 1
    pieces = [ids[0], ids[last], ids[:, 0], ids[:, last], ids[:, :, 0], ids[:, :, last]]
    return np.stack([p.reshape(-1) for p in pieces])


def trace_matrix(points):
    nodes = face_nodes(points)
    plane = points * points
    mat = np.zeros((6 * plane, points**3), np.float32)
    for face_index in range(6):
        mat[face_index * plane + np.arange(plane), nodes[face_index]] = 1.0
    return mat


def make_tables(neighbor, send_group, send_region, ghost_orient):
    elements = neighbor.shape[0]
    group_count = send_group.shape[2]
    region_count = send_region.shape[2]
    ghosts = 2 * group_count + 2 * region_count
    slots = jnp.arange(elements, dtype=jnp.int32)
    sources = jnp.arange(elements + ghosts, dtype=jnp.int32)
    gather = (neighbor.T[:, None, :] == sources[None, :, None]).astype(jnp.bfloat16)
    pick_group = (send_group[0][:, None, :] == slots[None, :, None]).astype(jnp.float32)
    pick_region = (send_region[0][:, None, :] == slots[None, :, None]).astype(jnp.float32)
    codes = (ghost_orient[0][None, :] == jnp.arange(8, dtype=jnp.int32)[:, None]).astype(
        jnp.float32
    )
    return gather, pick_group, pick_region, codes


def shift(block, axis, step):
    count = lax.axis_size(axis)
    if step > 0:
        pairs = [(i, i + 1) for i in range(count - 1)]
    else:
        pairs = [(i + 1, i) for i in range(count - 1)]
    return lax.ppermute(block, axis, pairs)


def region_exchange(region_out):
    count = lax.axis_size("region")
    odd = (lax.axis_index("region") % 2) == 1
    far_pairs = [(i, i + 1) for i in range(1, count - 1, 2)]
    far_pairs += [(i, i - 1) for i in range(2, count, 2)]
    near_pairs = [(i, i + 1) for i in range(0, count - 1, 2)]
    near_pairs += [(i + 1, i) for i in range(0, count - 1, 2)]
    near_recv = lax.ppermute(
        jnp.where(odd, region_out[0], region_out[1]), "region", near_pairs
    )
    far_recv = lax.ppermute(
        jnp.where(odd, region_out[1], region_out[0]), "region", far_pairs
    )
    return jnp.where(odd, near_recv, far_recv), jnp.where(odd, far_recv, near_recv)


def apply_level(current, stiffness, points, tables, extra=None, group_ghosts=None):
    gather, pick_group, pick_region, codes = tables
    plane = points * points
    cube = points**3
    elements = current.shape[1]
    select = jnp.asarray(trace_matrix(points))
    both = mm(jnp.concatenate([stiffness, select], axis=0), current)
    product = both[:cube]
    traces = both[cube:].reshape(6, plane, elements)
    region_out = jnp.einsum(
        "snj,sjk->snk", traces[2:4], pick_region, precision=HIGH,
        preferred_element_type=jnp.float32,
    )
    from_region_low, from_region_high = region_exchange(region_out)
    received = None
    if group_ghosts is None:
        group_out = jnp.einsum(
            "snj,sjk->snk", traces[0:2], pick_group, precision=HIGH,
            preferred_element_type=jnp.float32,
        )
        if extra is not None:
            group_out = jnp.concatenate([group_out, extra], axis=1)
        from_group_low = shift(group_out[1], "group", 1)
        from_group_high = shift(group_out[0], "group", -1)
        received = (from_group_low[plane:], from_group_high[plane:])
        group_ghosts = (from_group_low[:plane], from_group_high[:plane])
    raw = jnp.concatenate(
        [group_ghosts[0], group_ghosts[1], from_region_low, from_region_high], axis=1
    )
    turned = pick(jnp.asarray(orient_matrix(points)), raw).reshape(8, plane, -1)
    ghosts = jnp.sum(turned * codes[:, None, :], axis=0)
    swapped = traces[np.array([1, 0, 3, 2, 5, 4])]
    source = jnp.concatenate(
        [swapped, jnp.broadcast_to(ghosts[None], (6,) + ghosts.shape)], axis=2
    )
    outside = jnp.einsum(
        "fnq,fqe->fne", source, gather.astype(jnp.float32), precision=HIGH,
        preferred_element_type=jnp.float32,
    )
    jumps = (traces - outside).reshape(6 * plane, elements)
    return product + pick(select.T, jumps), received


def corner_values(window, ids, first_column, planes, vert_x):
    flat = ids.reshape(-1)
    plane_ids = flat // vert_x
    column = flat - plane_ids * vert_x - first_column
    on_plane = (plane_ids[None, :] == jnp.arange(planes, dtype=jnp.int32)[:, None]).astype(
        jnp.float32
    )
    on_column = (
        column[:, None] == jnp.arange(window.shape[1], dtype=jnp.int32)[None, :]
    ).astype(jnp.float32)
    picked = pick(window.T, on_plane)
    return jnp.sum(picked * on_column.T, axis=0).reshape(ids.shape)


def sine_basis(extent):
    ordinal = jnp.arange(1, extent + 1, dtype=jnp.int32)
    wrapped = ordinal[:, None] * ordinal[None, :] % (2 * (extent + 1))
    return math.sqrt(2.0 / (extent + 1)) * jnp.sin(
        wrapped.astype(jnp.float32) * (math.pi / (extent + 1))
    )


def spectrum(extent):
    cosine = jnp.cos(
        jnp.arange(1, extent + 1, dtype=jnp.int32).astype(jnp.float32) * (math.pi / (extent + 1))
    )
    return (2.0 - 2.0 * cosine, (4.0 + 2.0 * cosine) / 6.0)


def transform(volume, basis_z, basis_y, basis_x):
    turned = jnp.einsum("zyx,xk->zyk", volume, basis_x, precision=HIGHEST)
    turned = jnp.einsum("zyk,yj->zjk", turned, basis_y, precision=HIGHEST)
    return jnp.einsum("zjk,zi->ijk", turned, basis_z, precision=HIGHEST)


def coarse_solve(interior):
    depth_count, height_count, breadth_count = interior.shape
    basis_z, basis_y, basis_x = (
        sine_basis(depth_count),
        sine_basis(height_count),
        sine_basis(breadth_count),
    )
    stiff_z, mass_z = spectrum(depth_count)
    stiff_y, mass_y = spectrum(height_count)
    stiff_x, mass_x = spectrum(breadth_count)
    eigen_sum = (
        stiff_z[:, None, None] * mass_y[None, :, None] * mass_x[None, None, :]
        + mass_z[:, None, None] * stiff_y[None, :, None] * mass_x[None, None, :]
        + mass_z[:, None, None] * mass_y[None, :, None] * stiff_x[None, None, :]
    )
    return transform(
        transform(interior, basis_z, basis_y, basis_x) / eigen_sum, basis_z, basis_y, basis_x
    )


def gather_slab(local, width):
    index = lax.axis_index("group")
    vert_x = BX * width + 1
    full = lax.dynamic_update_slice(
        jnp.zeros((local.shape[0], vert_x), jnp.float32), local, (0, BX * index)
    )
    interior = full.reshape(BZ + 1, BY + 1, vert_x)[1:BZ, 1:BY, 1 : vert_x - 1]
    for bit in range(int(math.log2(width))):
        partner = [(i, i ^ (1 << bit)) for i in range(width)]
        interior = interior + lax.ppermute(interior, "group", partner)
    return interior


def body(
    right_side,
    stiff_fine,
    smooth_fine,
    restrict_fine,
    stiff_middle,
    smooth_middle,
    restrict_middle,
    neighbor,
    send_group,
    send_region,
    ghost_orient,
    corners,
):
    tables = make_tables(neighbor, send_group, send_region, ghost_orient)
    width_group = lax.axis_size("group")
    index = lax.axis_index("group")
    vert_x = width_group * BX + 1
    planes = (BZ + 1) * (BY + 1)
    corner_ids = corners.T
    sent_ids = jnp.einsum(
        "nj,sjk->snk", corner_ids.astype(jnp.float32), tables[1], precision=HIGHEST,
        preferred_element_type=jnp.float32,
    )

    smoothed = mm(smooth_fine, right_side)
    operated, received = apply_level(smoothed, stiff_fine, FINE_PTS, tables, extra=sent_ids)
    residual = right_side - operated
    neighbor_ids = jnp.round(jnp.concatenate(received, axis=1)).astype(jnp.int32)
    middle_rhs = mm(restrict_fine, residual)
    middle_fix = mm(smooth_middle, middle_rhs)
    middle_res = middle_rhs - apply_level(middle_fix, stiff_middle, MID_PTS, tables)[0]
    corner_terms = mm(restrict_middle, middle_res)

    plane_ids = corner_ids.reshape(-1) // vert_x
    column = corner_ids.reshape(-1) - plane_ids * vert_x - BX * index
    on_plane = (plane_ids[None, :] == jnp.arange(planes, dtype=jnp.int32)[:, None]).astype(
        jnp.float32
    )
    on_column = (column[:, None] == jnp.arange(BX + 1, dtype=jnp.int32)[None, :]).astype(
        jnp.float32
    )
    local = pick(on_plane, corner_terms.reshape(-1)[:, None] * on_column)
    interior = gather_slab(local, width_group)
    solved = coarse_solve(interior)
    padded = jnp.pad(solved, ((1, 1), (1, 1), (1 + BX, 1 + BX)))
    window = lax.dynamic_slice_in_dim(padded, BX * index, 3 * BX + 1, axis=2)
    window = window.reshape(planes, 3 * BX + 1)
    mine = window[:, BX : 2 * BX + 1]
    coarse_fix = corner_values(mine, corner_ids, BX * index, planes, vert_x)
    neighbor_fix = corner_values(window, neighbor_ids, BX * (index - 1), planes, vert_x)
    face_select = trace_matrix(MID_PTS).reshape(6, MID_PTS**2, MID_PTS**3)
    neighbor_corr = mm(restrict_middle.T, neighbor_fix)
    count = send_group.shape[2]
    low_valid = (index > 0).astype(jnp.float32)
    high_valid = (index < width_group - 1).astype(jnp.float32)
    group_ghosts = (
        mm(jnp.asarray(face_select[1]), neighbor_corr[:, :count]) * low_valid,
        mm(jnp.asarray(face_select[0]), neighbor_corr[:, count:]) * high_valid,
    )

    correction = mm(restrict_middle.T, coarse_fix)
    middle_corr = middle_fix + correction
    middle_left = middle_res - apply_level(
        correction, stiff_middle, MID_PTS, tables, group_ghosts=group_ghosts
    )[0]
    middle_post = middle_corr + mm(smooth_middle, middle_left)
    current = smoothed + mm(restrict_fine.T, middle_post)
    left_over = right_side - apply_level(current, stiff_fine, FINE_PTS, tables)[0]
    return current + mm(smooth_fine, left_over)


def solution(mesh):
    return jax.shard_map(
        body,
        mesh=mesh,
        in_specs=(
            P(None, ("region", "group")),
            P(),
            P(),
            P(),
            P(),
            P(),
            P(),
            P(("region", "group"), None),
            P(("region", "group"), None, None),
            P(("region", "group"), None, None),
            P(("region", "group"), None),
            P(("region", "group"), None),
        ),
        out_specs=P(None, ("region", "group")),
        check_vma=False,
    )
```

```python
import math

import jax
import jax.numpy as jnp
import numpy as np
from jax import lax
from jax.sharding import PartitionSpec as P

FINE_PTS = 6
MID_PTS = 3
BX = 2
BY = 8
BZ = 24


HIGHEST = lax.Precision.HIGHEST
HIGH = lax.Precision.HIGH
penalty_fine = 1.0
penalty_middle = 1.0


def mm(a, b):
    return jnp.dot(a, b, precision=HIGHEST, preferred_element_type=jnp.float32)


def pick(a, b):
    return jnp.dot(a, b, precision=HIGH, preferred_element_type=jnp.float32)


def orient_lookup(points):
    lookup = np.zeros((8, points * points), np.int32)
    for code_index in range(8):
        for row_index in range(points):
            for col_index in range(points):
                first_pos, second_pos = (row_index, col_index)
                if code_index >= 4:
                    first_pos, second_pos = (second_pos, first_pos)
                for rotation in range(code_index % 4):
                    first_pos, second_pos = (second_pos, points - 1 - first_pos)
                lookup[code_index, row_index * points + col_index] = first_pos * points + second_pos
    return lookup


def orient_matrix(points):
    lookup = orient_lookup(points)
    plane = points * points
    mat = np.zeros((8 * plane, plane), np.float32)
    for code_index in range(8):
        mat[code_index * plane + np.arange(plane), lookup[code_index]] = 1.0
    return mat


def face_nodes(points):
    ids = np.arange(points**3).reshape(points, points, points)
    last = points - 1
    pieces = [ids[0], ids[last], ids[:, 0], ids[:, last], ids[:, :, 0], ids[:, :, last]]
    return np.stack([p.reshape(-1) for p in pieces])


def trace_matrix(points):
    nodes = face_nodes(points)
    plane = points * points
    mat = np.zeros((6 * plane, points**3), np.float32)
    for face_index in range(6):
        mat[face_index * plane + np.arange(plane), nodes[face_index]] = 1.0
    return mat


def make_tables(neighbor, send_group, send_region, ghost_orient):
    elements = neighbor.shape[0]
    group_count = send_group.shape[2]
    region_count = send_region.shape[2]
    ghosts = 2 * group_count + 2 * region_count
    slots = jnp.arange(elements, dtype=jnp.int32)
    sources = jnp.arange(elements + ghosts, dtype=jnp.int32)
    gather = (neighbor.T[:, None, :] == sources[None, :, None]).astype(jnp.bfloat16)
    pick_group = (send_group[0][:, None, :] == slots[None, :, None]).astype(jnp.float32)
    pick_region = (send_region[0][:, None, :] == slots[None, :, None]).astype(jnp.float32)
    codes = (ghost_orient[0][None, :] == jnp.arange(8, dtype=jnp.int32)[:, None]).astype(
        jnp.float32
    )
    return gather, pick_group, pick_region, codes


def shift(block, axis, step):
    count = lax.axis_size(axis)
    if step > 0:
        pairs = [(i, i + 1) for i in range(count - 1)]
    else:
        pairs = [(i + 1, i) for i in range(count - 1)]
    return lax.ppermute(block, axis, pairs)


def region_exchange(region_out):
    count = lax.axis_size("region")
    odd = (lax.axis_index("region") % 2) == 1
    far_pairs = [(i, i + 1) for i in range(1, count - 1, 2)]
    far_pairs += [(i, i - 1) for i in range(2, count, 2)]
    near_pairs = [(i, i + 1) for i in range(0, count - 1, 2)]
    near_pairs += [(i + 1, i) for i in range(0, count - 1, 2)]
    near_recv = lax.ppermute(
        jnp.where(odd, region_out[0], region_out[1]), "region", near_pairs
    )
    far_recv = lax.ppermute(
        jnp.where(odd, region_out[1], region_out[0]), "region", far_pairs
    )
    return jnp.where(odd, near_recv, far_recv), jnp.where(odd, far_recv, near_recv)


def apply_level(current, stiffness, points, tables, extra=None, group_ghosts=None, sends=None):
    gather, pick_group, pick_region, codes = tables
    plane = points * points
    cube = points**3
    elements = current.shape[1]
    select = jnp.asarray(trace_matrix(points))
    both = mm(jnp.concatenate([stiffness, select], axis=0), current)
    product = both[:cube]
    traces = both[cube:].reshape(6, plane, elements)
    if sends is None:
        sends = (
            jnp.einsum(
                "snj,sjk->snk", traces[0:2], pick_group, precision=HIGH,
                preferred_element_type=jnp.float32,
            ),
            jnp.einsum(
                "snj,sjk->snk", traces[2:4], pick_region, precision=HIGH,
                preferred_element_type=jnp.float32,
            ),
        )
    region_out = sends[1]
    from_region_low, from_region_high = region_exchange(region_out)
    received = None
    if group_ghosts is None:
        group_out = sends[0]
        if extra is not None:
            group_out = jnp.concatenate([group_out, extra], axis=1)
        from_group_low = shift(group_out[1], "group", 1)
        from_group_high = shift(group_out[0], "group", -1)
        received = (from_group_low[plane:], from_group_high[plane:])
        group_ghosts = (from_group_low[:plane], from_group_high[:plane])
    raw = jnp.concatenate(
        [group_ghosts[0], group_ghosts[1], from_region_low, from_region_high], axis=1
    )
    turned = pick(jnp.asarray(orient_matrix(points)), raw).reshape(8, plane, -1)
    ghosts = jnp.sum(turned * codes[:, None, :], axis=0)
    swapped = traces[np.array([1, 0, 3, 2, 5, 4])]
    source = jnp.concatenate(
        [swapped, jnp.broadcast_to(ghosts[None], (6,) + ghosts.shape)], axis=2
    )
    outside = jnp.einsum(
        "fnq,fqe->fne", source, gather.astype(jnp.float32), precision=HIGH,
        preferred_element_type=jnp.float32,
    )
    jumps = (traces - outside).reshape(6 * plane, elements)
    return product + pick(select.T, jumps), received


def corner_values(window, ids, first_column, planes, vert_x):
    flat = ids.reshape(-1)
    plane_ids = flat // vert_x
    column = flat - plane_ids * vert_x - first_column
    on_plane = (plane_ids[None, :] == jnp.arange(planes, dtype=jnp.int32)[:, None]).astype(
        jnp.float32
    )
    on_column = (
        column[:, None] == jnp.arange(window.shape[1], dtype=jnp.int32)[None, :]
    ).astype(jnp.float32)
    picked = pick(window.T, on_plane)
    return jnp.sum(picked * on_column.T, axis=0).reshape(ids.shape)


def sine_basis(extent):
    ordinal = jnp.arange(1, extent + 1, dtype=jnp.int32)
    wrapped = ordinal[:, None] * ordinal[None, :] % (2 * (extent + 1))
    return math.sqrt(2.0 / (extent + 1)) * jnp.sin(
        wrapped.astype(jnp.float32) * (math.pi / (extent + 1))
    )


def spectrum(extent):
    cosine = jnp.cos(
        jnp.arange(1, extent + 1, dtype=jnp.int32).astype(jnp.float32) * (math.pi / (extent + 1))
    )
    return (2.0 - 2.0 * cosine, (4.0 + 2.0 * cosine) / 6.0)


def transform(volume, basis_z, basis_y, basis_x):
    turned = jnp.einsum("zyx,xk->zyk", volume, basis_x, precision=HIGHEST)
    turned = jnp.einsum("zyk,yj->zjk", turned, basis_y, precision=HIGHEST)
    return jnp.einsum("zjk,zi->ijk", turned, basis_z, precision=HIGHEST)


def coarse_solve(interior):
    depth_count, height_count, breadth_count = interior.shape
    basis_z, basis_y, basis_x = (
        sine_basis(depth_count),
        sine_basis(height_count),
        sine_basis(breadth_count),
    )
    stiff_z, mass_z = spectrum(depth_count)
    stiff_y, mass_y = spectrum(height_count)
    stiff_x, mass_x = spectrum(breadth_count)
    eigen_sum = (
        stiff_z[:, None, None] * mass_y[None, :, None] * mass_x[None, None, :]
        + mass_z[:, None, None] * stiff_y[None, :, None] * mass_x[None, None, :]
        + mass_z[:, None, None] * mass_y[None, :, None] * stiff_x[None, None, :]
    )
    return transform(
        transform(interior, basis_z, basis_y, basis_x) / eigen_sum, basis_z, basis_y, basis_x
    )


def gather_slab(local, width):
    index = lax.axis_index("group")
    vert_x = BX * width + 1
    full = lax.dynamic_update_slice(
        jnp.zeros((local.shape[0], vert_x), jnp.float32), local, (0, BX * index)
    )
    interior = full.reshape(BZ + 1, BY + 1, vert_x)[1:BZ, 1:BY, 1 : vert_x - 1]
    for bit in range(int(math.log2(width))):
        partner = [(i, i ^ (1 << bit)) for i in range(width)]
        interior = interior + lax.ppermute(interior, "group", partner)
    return interior


def body(
    right_side,
    stiff_fine,
    smooth_fine,
    restrict_fine,
    stiff_middle,
    smooth_middle,
    restrict_middle,
    neighbor,
    send_group,
    send_region,
    ghost_orient,
    corners,
):
    tables = make_tables(neighbor, send_group, send_region, ghost_orient)
    width_group = lax.axis_size("group")
    index = lax.axis_index("group")
    vert_x = width_group * BX + 1
    planes = (BZ + 1) * (BY + 1)
    corner_ids = corners.T
    sent_ids = jnp.einsum(
        "nj,sjk->snk", corner_ids.astype(jnp.float32), tables[1], precision=HIGHEST,
        preferred_element_type=jnp.float32,
    )

    face_smooth = mm(jnp.asarray(trace_matrix(FINE_PTS)), smooth_fine).reshape(6, -1, smooth_fine.shape[1])
    first_sends = tuple(
        jnp.einsum(
            "snj,sjk->snk",
            face_smooth[faces],
            jnp.einsum("jq,sqk->sjk", right_side, chosen, precision=HIGH,
                       preferred_element_type=jnp.float32),
            precision=HIGHEST,
            preferred_element_type=jnp.float32,
        )
        for faces, chosen in ((slice(0, 2), tables[1]), (slice(2, 4), tables[2]))
    )
    smoothed = mm(smooth_fine, right_side)
    operated, received = apply_level(
        smoothed, stiff_fine, FINE_PTS, tables, extra=sent_ids, sends=first_sends
    )
    residual = right_side - operated
    neighbor_ids = jnp.round(jnp.concatenate(received, axis=1)).astype(jnp.int32)
    middle_rhs = mm(restrict_fine, residual)
    middle_fix = mm(smooth_middle, middle_rhs)
    middle_res = middle_rhs - apply_level(middle_fix, stiff_middle, MID_PTS, tables)[0]
    corner_terms = mm(restrict_middle, middle_res)

    plane_ids = corner_ids.reshape(-1) // vert_x
    column = corner_ids.reshape(-1) - plane_ids * vert_x - BX * index
    on_plane = (plane_ids[None, :] == jnp.arange(planes, dtype=jnp.int32)[:, None]).astype(
        jnp.float32
    )
    on_column = (column[:, None] == jnp.arange(BX + 1, dtype=jnp.int32)[None, :]).astype(
        jnp.float32
    )
    local = pick(on_plane, corner_terms.reshape(-1)[:, None] * on_column)
    interior = gather_slab(local, width_group)
    solved = coarse_solve(interior)
    padded = jnp.pad(solved, ((1, 1), (1, 1), (1 + BX, 1 + BX)))
    window = lax.dynamic_slice_in_dim(padded, BX * index, 3 * BX + 1, axis=2)
    window = window.reshape(planes, 3 * BX + 1)
    mine = window[:, BX : 2 * BX + 1]
    coarse_fix = corner_values(mine, corner_ids, BX * index, planes, vert_x)
    neighbor_fix = corner_values(window, neighbor_ids, BX * (index - 1), planes, vert_x)
    face_select = trace_matrix(MID_PTS).reshape(6, MID_PTS**2, MID_PTS**3)
    neighbor_corr = mm(restrict_middle.T, neighbor_fix)
    count = send_group.shape[2]
    low_valid = (index > 0).astype(jnp.float32)
    high_valid = (index < width_group - 1).astype(jnp.float32)
    group_ghosts = (
        mm(jnp.asarray(face_select[1]), neighbor_corr[:, :count]) * low_valid,
        mm(jnp.asarray(face_select[0]), neighbor_corr[:, count:]) * high_valid,
    )

    correction = mm(restrict_middle.T, coarse_fix)
    middle_corr = middle_fix + correction
    middle_left = middle_res - apply_level(
        correction, stiff_middle, MID_PTS, tables, group_ghosts=group_ghosts
    )[0]
    middle_post = middle_corr + mm(smooth_middle, middle_left)
    current = smoothed + mm(restrict_fine.T, middle_post)
    left_over = right_side - apply_level(current, stiff_fine, FINE_PTS, tables)[0]
    return current + mm(smooth_fine, left_over)


def solution(mesh):
    return jax.shard_map(
        body,
        mesh=mesh,
        in_specs=(
            P(None, ("region", "group")),
            P(),
            P(),
            P(),
            P(),
            P(),
            P(),
            P(("region", "group"), None),
            P(("region", "group"), None, None),
            P(("region", "group"), None, None),
            P(("region", "group"), None),
            P(("region", "group"), None),
        ),
        out_specs=P(None, ("region", "group")),
        check_vma=False,
    )
```

```python
import math

import jax
import jax.numpy as jnp
import numpy as np
from jax import lax
from jax.sharding import PartitionSpec as P

FINE_PTS = 6
MID_PTS = 3
BX = 2
BY = 8
BZ = 24


HIGHEST = lax.Precision.HIGHEST
HIGH = lax.Precision.HIGH
penalty_fine = 1.0
penalty_middle = 1.0


def mm(a, b):
    return jnp.dot(a, b, precision=HIGHEST, preferred_element_type=jnp.float32)


def pick(a, b):
    return jnp.dot(a, b, precision=HIGH, preferred_element_type=jnp.float32)


def orient_lookup(points):
    lookup = np.zeros((8, points * points), np.int32)
    for code_index in range(8):
        for row_index in range(points):
            for col_index in range(points):
                first_pos, second_pos = (row_index, col_index)
                if code_index >= 4:
                    first_pos, second_pos = (second_pos, first_pos)
                for rotation in range(code_index % 4):
                    first_pos, second_pos = (second_pos, points - 1 - first_pos)
                lookup[code_index, row_index * points + col_index] = first_pos * points + second_pos
    return lookup


def orient_matrix(points):
    lookup = orient_lookup(points)
    plane = points * points
    mat = np.zeros((8 * plane, plane), np.float32)
    for code_index in range(8):
        mat[code_index * plane + np.arange(plane), lookup[code_index]] = 1.0
    return mat


def face_nodes(points):
    ids = np.arange(points**3).reshape(points, points, points)
    last = points - 1
    pieces = [ids[0], ids[last], ids[:, 0], ids[:, last], ids[:, :, 0], ids[:, :, last]]
    return np.stack([p.reshape(-1) for p in pieces])


def trace_matrix(points):
    nodes = face_nodes(points)
    plane = points * points
    mat = np.zeros((6 * plane, points**3), np.float32)
    for face_index in range(6):
        mat[face_index * plane + np.arange(plane), nodes[face_index]] = 1.0
    return mat


def make_tables(neighbor, send_group, send_region, ghost_orient):
    elements = neighbor.shape[0]
    group_count = send_group.shape[2]
    region_count = send_region.shape[2]
    ghosts = 2 * group_count + 2 * region_count
    slots = jnp.arange(elements, dtype=jnp.int32)
    sources = jnp.arange(elements + ghosts, dtype=jnp.int32)
    gather = (neighbor.T[:, None, :] == sources[None, :, None]).astype(jnp.bfloat16)
    pick_group = (send_group[0][:, None, :] == slots[None, :, None]).astype(jnp.float32)
    pick_region = (send_region[0][:, None, :] == slots[None, :, None]).astype(jnp.float32)
    codes = (ghost_orient[0][None, :] == jnp.arange(8, dtype=jnp.int32)[:, None]).astype(
        jnp.float32
    )
    return gather, pick_group, pick_region, codes


def shift(block, axis, step):
    count = lax.axis_size(axis)
    if step > 0:
        pairs = [(i, i + 1) for i in range(count - 1)]
    else:
        pairs = [(i + 1, i) for i in range(count - 1)]
    return lax.ppermute(block, axis, pairs)


def region_exchange(region_out, axis="region"):
    count = lax.axis_size(axis)
    odd = (lax.axis_index(axis) % 2) == 1
    far_pairs = [(i, i + 1) for i in range(1, count - 1, 2)]
    far_pairs += [(i, i - 1) for i in range(2, count, 2)]
    near_pairs = [(i, i + 1) for i in range(0, count - 1, 2)]
    near_pairs += [(i + 1, i) for i in range(0, count - 1, 2)]
    near_recv = lax.ppermute(
        jnp.where(odd, region_out[0], region_out[1]), axis, near_pairs
    )
    far_recv = lax.ppermute(
        jnp.where(odd, region_out[1], region_out[0]), axis, far_pairs
    )
    return jnp.where(odd, near_recv, far_recv), jnp.where(odd, far_recv, near_recv)


def apply_level(current, stiffness, points, tables, extra=None, group_ghosts=None):
    gather, pick_group, pick_region, codes = tables
    plane = points * points
    cube = points**3
    elements = current.shape[1]
    select = jnp.asarray(trace_matrix(points))
    both = mm(jnp.concatenate([stiffness, select], axis=0), current)
    product = both[:cube]
    traces = both[cube:].reshape(6, plane, elements)
    received = None
    if group_ghosts is None:
        group_out = jnp.einsum(
            "snj,sjk->snk", traces[0:2], pick_group, precision=HIGH,
            preferred_element_type=jnp.float32,
        )
        if extra is not None:
            group_out = jnp.concatenate([group_out, extra], axis=1)
        from_group_low, from_group_high = region_exchange(group_out, "group")
        received = (from_group_low[plane:], from_group_high[plane:])
        group_ghosts = (from_group_low[:plane], from_group_high[:plane])
    region_out = jnp.einsum(
        "snj,sjk->snk", traces[2:4], pick_region, precision=HIGH,
        preferred_element_type=jnp.float32,
    )
    from_region_low, from_region_high = region_exchange(region_out)
    raw = jnp.concatenate(
        [group_ghosts[0], group_ghosts[1], from_region_low, from_region_high], axis=1
    )
    turned = pick(jnp.asarray(orient_matrix(points)), raw).reshape(8, plane, -1)
    ghosts = jnp.sum(turned * codes[:, None, :], axis=0)
    swapped = traces[np.array([1, 0, 3, 2, 5, 4])]
    source = jnp.concatenate(
        [swapped, jnp.broadcast_to(ghosts[None], (6,) + ghosts.shape)], axis=2
    )
    outside = jnp.einsum(
        "fnq,fqe->fne", source, gather.astype(jnp.float32), precision=HIGH,
        preferred_element_type=jnp.float32,
    )
    jumps = (traces - outside).reshape(6 * plane, elements)
    return product + pick(select.T, jumps), received


def corner_values(window, ids, first_column, planes, vert_x):
    flat = ids.reshape(-1)
    plane_ids = flat // vert_x
    column = flat - plane_ids * vert_x - first_column
    on_plane = (plane_ids[None, :] == jnp.arange(planes, dtype=jnp.int32)[:, None]).astype(
        jnp.float32
    )
    on_column = (
        column[:, None] == jnp.arange(window.shape[1], dtype=jnp.int32)[None, :]
    ).astype(jnp.float32)
    picked = pick(window.T, on_plane)
    return jnp.sum(picked * on_column.T, axis=0).reshape(ids.shape)


def sine_basis(extent):
    ordinal = jnp.arange(1, extent + 1, dtype=jnp.int32)
    wrapped = ordinal[:, None] * ordinal[None, :] % (2 * (extent + 1))
    return math.sqrt(2.0 / (extent + 1)) * jnp.sin(
        wrapped.astype(jnp.float32) * (math.pi / (extent + 1))
    )


def spectrum(extent):
    cosine = jnp.cos(
        jnp.arange(1, extent + 1, dtype=jnp.int32).astype(jnp.float32) * (math.pi / (extent + 1))
    )
    return (2.0 - 2.0 * cosine, (4.0 + 2.0 * cosine) / 6.0)


def transform(volume, basis_z, basis_y, basis_x):
    turned = jnp.einsum("zyx,xk->zyk", volume, basis_x, precision=HIGHEST)
    turned = jnp.einsum("zyk,yj->zjk", turned, basis_y, precision=HIGHEST)
    return jnp.einsum("zjk,zi->ijk", turned, basis_z, precision=HIGHEST)


def coarse_solve(interior):
    depth_count, height_count, breadth_count = interior.shape
    basis_z, basis_y, basis_x = (
        sine_basis(depth_count),
        sine_basis(height_count),
        sine_basis(breadth_count),
    )
    stiff_z, mass_z = spectrum(depth_count)
    stiff_y, mass_y = spectrum(height_count)
    stiff_x, mass_x = spectrum(breadth_count)
    eigen_sum = (
        stiff_z[:, None, None] * mass_y[None, :, None] * mass_x[None, None, :]
        + mass_z[:, None, None] * stiff_y[None, :, None] * mass_x[None, None, :]
        + mass_z[:, None, None] * mass_y[None, :, None] * stiff_x[None, None, :]
    )
    return transform(
        transform(interior, basis_z, basis_y, basis_x) / eigen_sum, basis_z, basis_y, basis_x
    )


def gather_slab(local, width):
    index = lax.axis_index("group")
    vert_x = BX * width + 1
    full = lax.dynamic_update_slice(
        jnp.zeros((local.shape[0], vert_x), jnp.float32), local, (0, BX * index)
    )
    interior = full.reshape(BZ + 1, BY + 1, vert_x)[1:BZ, 1:BY, 1 : vert_x - 1]
    for bit in range(int(math.log2(width))):
        partner = [(i, i ^ (1 << bit)) for i in range(width)]
        interior = interior + lax.ppermute(interior, "group", partner)
    return interior


def body(
    right_side,
    stiff_fine,
    smooth_fine,
    restrict_fine,
    stiff_middle,
    smooth_middle,
    restrict_middle,
    neighbor,
    send_group,
    send_region,
    ghost_orient,
    corners,
):
    tables = make_tables(neighbor, send_group, send_region, ghost_orient)
    width_group = lax.axis_size("group")
    index = lax.axis_index("group")
    vert_x = width_group * BX + 1
    planes = (BZ + 1) * (BY + 1)
    corner_ids = corners.T
    sent_ids = jnp.einsum(
        "nj,sjk->snk", corner_ids.astype(jnp.float32), tables[1], precision=HIGHEST,
        preferred_element_type=jnp.float32,
    )

    smoothed = mm(smooth_fine, right_side)
    operated, received = apply_level(smoothed, stiff_fine, FINE_PTS, tables, extra=sent_ids)
    residual = right_side - operated
    neighbor_ids = jnp.round(jnp.concatenate(received, axis=1)).astype(jnp.int32)
    middle_rhs = mm(restrict_fine, residual)
    middle_fix = mm(smooth_middle, middle_rhs)
    middle_res = middle_rhs - apply_level(middle_fix, stiff_middle, MID_PTS, tables)[0]
    corner_terms = mm(restrict_middle, middle_res)

    plane_ids = corner_ids.reshape(-1) // vert_x
    column = corner_ids.reshape(-1) - plane_ids * vert_x - BX * index
    on_plane = (plane_ids[None, :] == jnp.arange(planes, dtype=jnp.int32)[:, None]).astype(
        jnp.float32
    )
    on_column = (column[:, None] == jnp.arange(BX + 1, dtype=jnp.int32)[None, :]).astype(
        jnp.float32
    )
    local = pick(on_plane, corner_terms.reshape(-1)[:, None] * on_column)
    interior = gather_slab(local, width_group)
    solved = coarse_solve(interior)
    padded = jnp.pad(solved, ((1, 1), (1, 1), (1 + BX, 1 + BX)))
    window = lax.dynamic_slice_in_dim(padded, BX * index, 3 * BX + 1, axis=2)
    window = window.reshape(planes, 3 * BX + 1)
    mine = window[:, BX : 2 * BX + 1]
    coarse_fix = corner_values(mine, corner_ids, BX * index, planes, vert_x)
    neighbor_fix = corner_values(window, neighbor_ids, BX * (index - 1), planes, vert_x)
    face_select = trace_matrix(MID_PTS).reshape(6, MID_PTS**2, MID_PTS**3)
    neighbor_corr = mm(restrict_middle.T, neighbor_fix)
    count = send_group.shape[2]
    low_valid = (index > 0).astype(jnp.float32)
    high_valid = (index < width_group - 1).astype(jnp.float32)
    group_ghosts = (
        mm(jnp.asarray(face_select[1]), neighbor_corr[:, :count]) * low_valid,
        mm(jnp.asarray(face_select[0]), neighbor_corr[:, count:]) * high_valid,
    )

    correction = mm(restrict_middle.T, coarse_fix)
    middle_corr = middle_fix + correction
    middle_left = middle_res - apply_level(
        correction, stiff_middle, MID_PTS, tables, group_ghosts=group_ghosts
    )[0]
    middle_post = middle_corr + mm(smooth_middle, middle_left)
    current = smoothed + mm(restrict_fine.T, middle_post)
    left_over = right_side - apply_level(current, stiff_fine, FINE_PTS, tables)[0]
    return current + mm(smooth_fine, left_over)


def solution(mesh):
    return jax.shard_map(
        body,
        mesh=mesh,
        in_specs=(
            P(None, ("region", "group")),
            P(),
            P(),
            P(),
            P(),
            P(),
            P(),
            P(("region", "group"), None),
            P(("region", "group"), None, None),
            P(("region", "group"), None, None),
            P(("region", "group"), None),
            P(("region", "group"), None),
        ),
        out_specs=P(None, ("region", "group")),
        check_vma=False,
    )
```

```python
import math

import jax
import jax.numpy as jnp
import numpy as np
from jax import lax
from jax.sharding import PartitionSpec as P

FINE_PTS = 6
MID_PTS = 3
BX = 2
BY = 8
BZ = 24


HIGHEST = lax.Precision.HIGHEST
HIGH = lax.Precision.HIGH
penalty_fine = 1.0
penalty_middle = 1.0


def mm(a, b):
    return jnp.dot(a, b, precision=HIGHEST, preferred_element_type=jnp.float32)


def pick(a, b):
    return jnp.dot(a, b, precision=HIGH, preferred_element_type=jnp.float32)


def orient_lookup(points):
    lookup = np.zeros((8, points * points), np.int32)
    for code_index in range(8):
        for row_index in range(points):
            for col_index in range(points):
                first_pos, second_pos = (row_index, col_index)
                if code_index >= 4:
                    first_pos, second_pos = (second_pos, first_pos)
                for rotation in range(code_index % 4):
                    first_pos, second_pos = (second_pos, points - 1 - first_pos)
                lookup[code_index, row_index * points + col_index] = first_pos * points + second_pos
    return lookup


def orient_matrix(points):
    lookup = orient_lookup(points)
    plane = points * points
    mat = np.zeros((8 * plane, plane), np.float32)
    for code_index in range(8):
        mat[code_index * plane + np.arange(plane), lookup[code_index]] = 1.0
    return mat


def face_nodes(points):
    ids = np.arange(points**3).reshape(points, points, points)
    last = points - 1
    pieces = [ids[0], ids[last], ids[:, 0], ids[:, last], ids[:, :, 0], ids[:, :, last]]
    return np.stack([p.reshape(-1) for p in pieces])


def trace_matrix(points):
    nodes = face_nodes(points)
    plane = points * points
    mat = np.zeros((6 * plane, points**3), np.float32)
    for face_index in range(6):
        mat[face_index * plane + np.arange(plane), nodes[face_index]] = 1.0
    return mat


def make_tables(neighbor, send_group, send_region, ghost_orient):
    elements = neighbor.shape[0]
    group_count = send_group.shape[2]
    region_count = send_region.shape[2]
    ghosts = 2 * group_count + 2 * region_count
    slots = jnp.arange(elements, dtype=jnp.int32)
    sources = jnp.arange(elements + ghosts, dtype=jnp.int32)
    gather = (neighbor.T[:, None, :] == sources[None, :, None]).astype(jnp.bfloat16)
    pick_group = (send_group[0][:, None, :] == slots[None, :, None]).astype(jnp.float32)
    pick_region = (send_region[0][:, None, :] == slots[None, :, None]).astype(jnp.float32)
    codes = (ghost_orient[0][None, :] == jnp.arange(8, dtype=jnp.int32)[:, None]).astype(
        jnp.float32
    )
    return gather, pick_group, pick_region, codes


def shift(block, axis, step):
    count = lax.axis_size(axis)
    if step > 0:
        pairs = [(i, i + 1) for i in range(count - 1)]
    else:
        pairs = [(i + 1, i) for i in range(count - 1)]
    return lax.ppermute(block, axis, pairs)


def region_exchange(region_out):
    count = lax.axis_size("region")
    odd = (lax.axis_index("region") % 2) == 1
    far_pairs = [(i, i + 1) for i in range(1, count - 1, 2)]
    far_pairs += [(i, i - 1) for i in range(2, count, 2)]
    near_pairs = [(i, i + 1) for i in range(0, count - 1, 2)]
    near_pairs += [(i + 1, i) for i in range(0, count - 1, 2)]
    near_recv = lax.ppermute(
        jnp.where(odd, region_out[0], region_out[1]), "region", near_pairs
    )
    far_recv = lax.ppermute(
        jnp.where(odd, region_out[1], region_out[0]), "region", far_pairs
    )
    return jnp.where(odd, near_recv, far_recv), jnp.where(odd, far_recv, near_recv)


def apply_level(current, stiffness, points, tables, extra=None, group_ghosts=None):
    gather, pick_group, pick_region, codes = tables
    plane = points * points
    cube = points**3
    elements = current.shape[1]
    select = jnp.asarray(trace_matrix(points))
    both = mm(jnp.concatenate([stiffness, select], axis=0), current)
    product = both[:cube]
    traces = both[cube:].reshape(6, plane, elements)
    region_out = jnp.einsum(
        "snj,sjk->snk", traces[2:4], pick_region, precision=HIGH,
        preferred_element_type=jnp.float32,
    )
    from_region_low, from_region_high = region_exchange(region_out)
    received = None
    if group_ghosts is None:
        group_out = jnp.einsum(
            "snj,sjk->snk", traces[0:2], pick_group, precision=HIGH,
            preferred_element_type=jnp.float32,
        )
        if extra is not None:
            group_out = jnp.concatenate([group_out, extra], axis=1)
        from_group_low = shift(group_out[1], "group", 1)
        from_group_high = shift(group_out[0], "group", -1)
        received = (from_group_low[plane:], from_group_high[plane:])
        group_ghosts = (from_group_low[:plane], from_group_high[:plane])
    raw = jnp.concatenate(
        [group_ghosts[0], group_ghosts[1], from_region_low, from_region_high], axis=1
    )
    turned = pick(jnp.asarray(orient_matrix(points)), raw).reshape(8, plane, -1)
    ghosts = jnp.sum(turned * codes[:, None, :], axis=0)
    swapped = traces[np.array([1, 0, 3, 2, 5, 4])]
    source = jnp.concatenate(
        [swapped, jnp.broadcast_to(ghosts[None], (6,) + ghosts.shape)], axis=2
    )
    outside = jnp.einsum(
        "fnq,fqe->fne", source, gather.astype(jnp.float32), precision=HIGH,
        preferred_element_type=jnp.float32,
    )
    jumps = (traces - outside).reshape(6 * plane, elements)
    return product + pick(select.T, jumps), received


def corner_values(window, ids, first_column, planes, vert_x):
    flat = ids.reshape(-1)
    plane_ids = flat // vert_x
    column = flat - plane_ids * vert_x - first_column
    on_plane = (plane_ids[None, :] == jnp.arange(planes, dtype=jnp.int32)[:, None]).astype(
        jnp.float32
    )
    on_column = (
        column[:, None] == jnp.arange(window.shape[1], dtype=jnp.int32)[None, :]
    ).astype(jnp.float32)
    picked = pick(window.T, on_plane)
    return jnp.sum(picked * on_column.T, axis=0).reshape(ids.shape)


def sine_basis(extent):
    ordinal = jnp.arange(1, extent + 1, dtype=jnp.int32)
    wrapped = ordinal[:, None] * ordinal[None, :] % (2 * (extent + 1))
    return math.sqrt(2.0 / (extent + 1)) * jnp.sin(
        wrapped.astype(jnp.float32) * (math.pi / (extent + 1))
    )


def spectrum(extent):
    cosine = jnp.cos(
        jnp.arange(1, extent + 1, dtype=jnp.int32).astype(jnp.float32) * (math.pi / (extent + 1))
    )
    return (2.0 - 2.0 * cosine, (4.0 + 2.0 * cosine) / 6.0)


def transform(volume, basis_z, basis_y, basis_x):
    turned = jnp.einsum("zyx,xk->zyk", volume, basis_x, precision=HIGH)
    turned = jnp.einsum("zyk,yj->zjk", turned, basis_y, precision=HIGH)
    return jnp.einsum("zjk,zi->ijk", turned, basis_z, precision=HIGH)


def coarse_solve(interior):
    depth_count, height_count, breadth_count = interior.shape
    basis_z, basis_y, basis_x = (
        sine_basis(depth_count),
        sine_basis(height_count),
        sine_basis(breadth_count),
    )
    stiff_z, mass_z = spectrum(depth_count)
    stiff_y, mass_y = spectrum(height_count)
    stiff_x, mass_x = spectrum(breadth_count)
    eigen_sum = (
        stiff_z[:, None, None] * mass_y[None, :, None] * mass_x[None, None, :]
        + mass_z[:, None, None] * stiff_y[None, :, None] * mass_x[None, None, :]
        + mass_z[:, None, None] * mass_y[None, :, None] * stiff_x[None, None, :]
    )
    return transform(
        transform(interior, basis_z, basis_y, basis_x) / eigen_sum, basis_z, basis_y, basis_x
    )


def gather_slab(local, width):
    index = lax.axis_index("group")
    vert_x = BX * width + 1
    full = lax.dynamic_update_slice(
        jnp.zeros((local.shape[0], vert_x), jnp.float32), local, (0, BX * index)
    )
    interior = full.reshape(BZ + 1, BY + 1, vert_x)[1:BZ, 1:BY, 1 : vert_x - 1]
    for bit in range(int(math.log2(width))):
        partner = [(i, i ^ (1 << bit)) for i in range(width)]
        interior = interior + lax.ppermute(interior, "group", partner)
    return interior


def body(
    right_side,
    stiff_fine,
    smooth_fine,
    restrict_fine,
    stiff_middle,
    smooth_middle,
    restrict_middle,
    neighbor,
    send_group,
    send_region,
    ghost_orient,
    corners,
):
    tables = make_tables(neighbor, send_group, send_region, ghost_orient)
    width_group = lax.axis_size("group")
    index = lax.axis_index("group")
    vert_x = width_group * BX + 1
    planes = (BZ + 1) * (BY + 1)
    corner_ids = corners.T
    sent_ids = jnp.einsum(
        "nj,sjk->snk", corner_ids.astype(jnp.float32), tables[1], precision=HIGHEST,
        preferred_element_type=jnp.float32,
    )

    smoothed = mm(smooth_fine, right_side)
    operated, received = apply_level(smoothed, stiff_fine, FINE_PTS, tables, extra=sent_ids)
    residual = right_side - operated
    neighbor_ids = jnp.round(jnp.concatenate(received, axis=1)).astype(jnp.int32)
    middle_rhs = mm(restrict_fine, residual)
    middle_fix = mm(smooth_middle, middle_rhs)
    middle_res = middle_rhs - apply_level(middle_fix, stiff_middle, MID_PTS, tables)[0]
    corner_terms = mm(restrict_middle, middle_res)

    plane_ids = corner_ids.reshape(-1) // vert_x
    column = corner_ids.reshape(-1) - plane_ids * vert_x - BX * index
    on_plane = (plane_ids[None, :] == jnp.arange(planes, dtype=jnp.int32)[:, None]).astype(
        jnp.float32
    )
    on_column = (column[:, None] == jnp.arange(BX + 1, dtype=jnp.int32)[None, :]).astype(
        jnp.float32
    )
    local = pick(on_plane, corner_terms.reshape(-1)[:, None] * on_column)
    interior = gather_slab(local, width_group)
    solved = coarse_solve(interior)
    padded = jnp.pad(solved, ((1, 1), (1, 1), (1 + BX, 1 + BX)))
    window = lax.dynamic_slice_in_dim(padded, BX * index, 3 * BX + 1, axis=2)
    window = window.reshape(planes, 3 * BX + 1)
    mine = window[:, BX : 2 * BX + 1]
    coarse_fix = corner_values(mine, corner_ids, BX * index, planes, vert_x)
    neighbor_fix = corner_values(window, neighbor_ids, BX * (index - 1), planes, vert_x)
    face_select = trace_matrix(MID_PTS).reshape(6, MID_PTS**2, MID_PTS**3)
    neighbor_corr = mm(restrict_middle.T, neighbor_fix)
    count = send_group.shape[2]
    low_valid = (index > 0).astype(jnp.float32)
    high_valid = (index < width_group - 1).astype(jnp.float32)
    group_ghosts = (
        mm(jnp.asarray(face_select[1]), neighbor_corr[:, :count]) * low_valid,
        mm(jnp.asarray(face_select[0]), neighbor_corr[:, count:]) * high_valid,
    )

    correction = mm(restrict_middle.T, coarse_fix)
    middle_corr = middle_fix + correction
    middle_left = middle_res - apply_level(
        correction, stiff_middle, MID_PTS, tables, group_ghosts=group_ghosts
    )[0]
    middle_post = middle_corr + mm(smooth_middle, middle_left)
    current = smoothed + mm(restrict_fine.T, middle_post)
    left_over = right_side - apply_level(current, stiff_fine, FINE_PTS, tables)[0]
    return current + mm(smooth_fine, left_over)


def solution(mesh):
    return jax.shard_map(
        body,
        mesh=mesh,
        in_specs=(
            P(None, ("region", "group")),
            P(),
            P(),
            P(),
            P(),
            P(),
            P(),
            P(("region", "group"), None),
            P(("region", "group"), None, None),
            P(("region", "group"), None, None),
            P(("region", "group"), None),
            P(("region", "group"), None),
        ),
        out_specs=P(None, ("region", "group")),
        check_vma=False,
    )
```
